512 devices in a mesh: section: 4 (over x), expert: 16 (over z), rep: 8 (over y, core).
Axes of the slice: x: 4, y: 4, z: 16, core: 2. Of those that a mesh axis runs over, the one named last changes fastest.
Arguments:
- tokens: bfloat16 [4, 2048, 4096], P('section', 'expert', 'rep'), may hold values from -6 to 6
- expert_ids: int32 [4, 2048, 2], P('section', 'expert'), may hold values from 0 to 15, all different within a row; in each aligned block of 128 rows (0 to 127, 128 to 255, ..., all dimensions but the last counted through in order) at most 20 rows name the same one
- route_weight: float32 [4, 2048, 2], P('section', 'expert'), may hold values from 0.05 to 0.5
- language: int32 [4, 2048], P('section', 'expert'), may hold values from 0 to 3
- capacity: int32 [4, 16], replicated, may hold values from 0 to 7
- spill_table: int32 [4, 16], P('section'), may hold values from 0 to 15, as said below
- w_gate: bfloat16 [4, 16, 4096, 1024], P('section', 'expert', None, 'rep'), may hold values from -0.09375 to 0.09375
- w_up: bfloat16 [4, 16, 4096, 1024], P('section', 'expert', None, 'rep'), may hold values from -0.09375 to 0.09375
- w_down: bfloat16 [4, 16, 1024, 4096], P('section', 'expert', None, 'rep'), may hold values from -0.1875 to 0.1875
Outputs:
- next_rows: bfloat16 [4, 2048, 4096], P('section', 'expert', 'rep')
The draws below stay inside these ranges and needn't reach their ends.
Inputs may be any that keep to these rules, and one draw needn't show every extreme that they name: `expert_ids`: each token names 2 different experts. Among the tokens of one index of expert (aligned blocks of 128 rows, sections in order) no expert is named by more than 20 tokens, a bound that some block reaches. `spill_table`: in each section's row every expert names another expert, and every expert is named by exactly one; each row is one cycle through all 16.
All inputs are finite; a program needn't handle non-finite values.
Results may differ from the reference program's by a relative error of at most 0.0057.
Values may be sent and summed in bfloat16 or wider, within the bound.
No kernel may reach another device: no remote copies, remote signals or barrier semaphores. Data moves between devices by JAX's collectives and lax.ppermute only.
A program may use at most 64 MiB of HBM per device.

```python
import math
import jax
import jax.numpy as jnp
import numpy as np
from jax import lax

D = 4096
FF = 1024
LANGS = 4
TOK_DEV = 128
EXPERTS = 16
TOP = 2
TOKENS = 2048
MOST = 20
CAP_TOP = 8
N_SECTION = 4
N_EXPERT = 16


def one_cycle(section_key):
    order = jax.random.permutation(section_key, EXPERTS).astype(jnp.int32)
    return jnp.zeros((EXPERTS,), jnp.int32).at[order].set(jnp.roll(order, -1))


def draw_spill_table(key, part):
    section_keys = jax.random.split(jax.random.fold_in(key, 7), N_SECTION)
    return jax.vmap(one_cycle)(section_keys).astype(jnp.int32)


def place_ends(drawn, key, smallest, largest):
    place = [jax.random.randint(jax.random.fold_in(key, axis), (), 0, length) for axis, length in enumerate(drawn.shape)]
    widest = drawn.shape.index(max(drawn.shape))
    beside = place[:widest] + [(place[widest] + 1) % drawn.shape[widest]] + place[widest + 1:]
    return drawn.at[tuple(place)].set(smallest).at[tuple(beside)].set(largest)


def level_of(key, shape, shards, least, top_value):
    gain = 1.0
    for dim, parts in shards:
        steps = jax.random.uniform(jax.random.fold_in(jax.random.fold_in(key, 6), dim), (parts,), jnp.float32, least / len(shards), top_value / len(shards))
        gain = gain * jnp.repeat(jnp.exp(steps), shape[dim] // parts).reshape((-1,) + (1,) * (len(shape) - 1 - dim))
    return gain


def routed_block(stream_key, own, number, rows, amount, top, most, slope):
    order = jax.random.permutation(stream_key, amount)
    packed, usual = load_shares(amount, rows * top, most, slope, True), load_shares(amount, rows * top, most, slope, False)
    places = jnp.arange(amount)

    def named(sizes, offset_by):
        used = int((sizes > 0).sum())
        fixed = max(1, used // 4)
        passed = fixed + (places - fixed + offset_by * (used - fixed)) % max(1, amount - fixed)
        return jnp.zeros((amount,), jnp.int32).at[order[jnp.where(places < fixed, places, passed)]].set(jnp.asarray(sizes, jnp.int32))

    sizes = jnp.where(number % 4 == 0, named(packed, number // 4), named(usual, number - number // 4 - 1))
    mixed = jax.random.permutation(jax.random.fold_in(own, 3), amount)
    donor, sink = mixed[0:amount // 2 * 2:2], mixed[1:amount // 2 * 2:2]
    slack = jnp.minimum(sizes[donor] - 1, most - sizes[sink]) // 2
    slack = jnp.where((donor == order[0]) | (sink == order[0]) | (sizes[sink] == 0), 0, jnp.maximum(slack, 0))
    passed = jax.random.randint(jax.random.fold_in(own, 4), (amount // 2,), 0, 1 << 20) % (slack + 1)
    sizes = sizes.at[donor].add(-passed).at[sink].add(passed)
    members = jnp.searchsorted(jnp.cumsum(sizes), jnp.arange(rows * top), side="right").astype(jnp.int32)
    grid = members.reshape(top, rows).T
    grid = grid[jax.random.permutation(jax.random.fold_in(own, 1), rows)]
    offset_by = jax.random.randint(jax.random.fold_in(own, 2), (rows, 1), 0, top)
    return jnp.take_along_axis(grid, (jnp.arange(top)[None, :] + offset_by) % top, axis=1)


def load_shares(number_of, total, reach, slope, full):
    weights = [(1 << 20) // math.isqrt(rank ** slope) + 1 for rank in range(1, number_of + 1)]
    largest = reach if full else min(reach, max(-(-total // number_of), total * weights[0] // sum(weights)))
    least = 1 if total - largest >= number_of - 1 else 0
    given, rest = [largest] + [least] * (number_of - 1), total - largest - least * (number_of - 1)
    while rest > 0:
        candidates = [i for i in range(1, number_of) if given[i] < largest] or [i for i in range(1, number_of) if given[i] < reach]
        mass, budget = sum([weights[i] for i in candidates]), rest
        for i in candidates:
            more = min(reach - given[i], max(1, budget * weights[i] // mass), rest)
            given[i] = given[i] + more
            rest = rest - more
    return np.array(given)


def scatter_about(key, extent, scale, reach, cuts=(), held_as=jnp.bfloat16):
    values = scale * jax.random.normal(key, extent, jnp.float32)
    if cuts:
        values = values * level_of(key, extent, cuts, -0.22, 0.18)
    return jnp.clip(values, -reach, reach).astype(held_as)


def setup_inputs(seed: int = 0) -> dict:
    seeds = jax.random.split(jax.random.key(seed), 10)
    tokens = scatter_about(seeds[0], (N_SECTION, TOKENS, D), 1.0, 6.0, ((0, 4), (1, 16), (2, 8)))
    expert_ids_keys = jax.random.split(jax.random.fold_in(seeds[1], 1), N_SECTION * TOKENS // TOK_DEV)
    expert_ids_turns = jax.random.permutation(jax.random.fold_in(seeds[1], 3), N_SECTION * TOKENS // TOK_DEV)
    expert_ids = jax.vmap(lambda own, number: routed_block(jax.random.fold_in(seeds[1], 2), own, number, TOK_DEV, EXPERTS, TOP, MOST, 1))(expert_ids_keys, expert_ids_turns).reshape((N_SECTION, TOKENS, TOP))
    route_weight = jnp.clip(0.05 + 0.45 * jax.random.uniform(seeds[2], (N_SECTION, TOKENS, TOP), jnp.float32) ** level_of(seeds[2], (N_SECTION, TOKENS, TOP), ((0, 4), (1, 16)), -0.2, 0.2), 0.05, 0.5)
    language = place_ends(jax.random.randint(seeds[3], (N_SECTION, TOKENS), 0, LANGS), jax.random.fold_in(seeds[3], 1), 0, LANGS - 1).astype(jnp.int32)
    capacity = place_ends(jax.random.randint(seeds[4], (LANGS, EXPERTS), 0, CAP_TOP), jax.random.fold_in(seeds[4], 1), 0, CAP_TOP - 1).astype(jnp.int32)
    spill_table = draw_spill_table(jax.random.fold_in(seeds[9], 71), 0)
    w_gate = scatter_about(seeds[6], (N_SECTION, EXPERTS, D, FF), D ** -0.5, 0.09375, ((0, 4), (1, 16), (3, 8)))
    w_up = scatter_about(seeds[7], (N_SECTION, EXPERTS, D, FF), D ** -0.5, 0.09375, ((0, 4), (1, 16), (3, 8)))
    w_down = scatter_about(seeds[8], (N_SECTION, EXPERTS, FF, D), FF ** -0.5, 0.1875, ((0, 4), (1, 16), (3, 8)))
    return dict(tokens=tokens, expert_ids=expert_ids, route_weight=route_weight, language=language, capacity=capacity, spill_table=spill_table, w_gate=w_gate, w_up=w_up, w_down=w_down)


group_rows = 128


def admission(chosen, language, capacity):
    expert_count = capacity.shape[1]
    lang_count = capacity.shape[0]
    hit_table = jnp.sum((chosen[:, :, None] == jnp.arange(expert_count, dtype=jnp.int32)[None, None, :]).astype(jnp.int32), axis=1).astype(jnp.int32)
    lang_hot = (language[:, None] == jnp.arange(lang_count, dtype=jnp.int32)[None, :]).astype(jnp.int32)
    lang_hits = lang_hot[:, :, None] * hit_table[:, None, :]
    before = (jnp.cumsum(lang_hits, axis=0) - lang_hits).astype(jnp.int32)
    place_rank = jnp.sum(before * lang_hot[:, :, None], axis=1).astype(jnp.int32)
    allowance = jnp.sum(lang_hot[:, :, None] * capacity[None, :, :], axis=1).astype(jnp.int32)
    return hit_table * (place_rank < allowance).astype(jnp.int32)


def route_section(chosen, language, capacity, spill_row):
    admitted = jax.vmap(lambda ids_block, lang_block: admission(ids_block, lang_block, capacity))(
        chosen.reshape(N_EXPERT, TOK_DEV, TOP), language.reshape(N_EXPERT, TOK_DEV))
    admitted = admitted.reshape(TOKENS, EXPERTS)
    row_kept = jnp.take_along_axis(admitted, chosen, axis=1)
    return jnp.where(row_kept > 0, chosen, spill_row[chosen]).astype(jnp.int32)


def expert_section(rows_in, target, w_gate, w_up, w_down):
    total_rows = TOKENS * TOP
    expanded = jnp.repeat(rows_in, TOP, axis=0)
    flat_target = target.reshape(total_rows).astype(jnp.int32)
    order = jnp.argsort(flat_target, stable=True).astype(jnp.int32)
    sorted_target = flat_target[order]
    counts = jnp.sum((flat_target[:, None] == jnp.arange(EXPERTS, dtype=jnp.int32)[None, :]).astype(jnp.int32), axis=0).astype(jnp.int32)
    padded = ((counts + group_rows - 1) // group_rows * group_rows).astype(jnp.int32)
    ends = jnp.cumsum(padded).astype(jnp.int32)
    starts = ends - padded
    firsts = (jnp.cumsum(counts) - counts).astype(jnp.int32)
    placement = (starts[sorted_target] + jnp.arange(total_rows, dtype=jnp.int32) - firsts[sorted_target]).astype(jnp.int32)
    groups = total_rows // group_rows + EXPERTS + 1
    buffer = jnp.zeros((groups * group_rows, D), rows_in.dtype).at[placement].set(expanded[order])
    group_starts = (jnp.arange(groups, dtype=jnp.int32) * group_rows)[:, None]
    owners = jnp.minimum(jnp.sum((ends[None, :] <= group_starts).astype(jnp.int32), axis=1), EXPERTS - 1).astype(jnp.int32)

    def apply_group(operands):
        group, owner = operands
        gate_proj = jnp.dot(group, w_gate[owner], preferred_element_type=jnp.float32)
        up_proj = jnp.dot(group, w_up[owner], preferred_element_type=jnp.float32)
        activated = (jax.nn.silu(gate_proj) * up_proj).astype(jnp.bfloat16)
        return jnp.dot(activated, w_down[owner], preferred_element_type=jnp.float32).astype(jnp.bfloat16)

    results = lax.map(apply_group, (buffer.reshape(groups, group_rows, D), owners))
    in_order = results.reshape(groups * group_rows, D)[placement]
    outputs = jnp.zeros((total_rows, D), in_order.dtype).at[order].set(in_order)
    return outputs.reshape(TOKENS, TOP, D)


def reference(tokens, expert_ids, route_weight, language, capacity, spill_table, w_gate, w_up, w_down):
    sections = []
    for section_index in range(N_SECTION):
        target = route_section(expert_ids[section_index], language[section_index], capacity, spill_table[section_index])
        expert_out = expert_section(tokens[section_index], target, w_gate[section_index], w_up[section_index], w_down[section_index])
        combined = jnp.sum(route_weight[section_index][:, :, None] * expert_out.astype(jnp.float32), axis=1).astype(jnp.bfloat16)
        sections.append(combined)
    combined_all = jnp.stack(sections)
    return jnp.roll(combined_all, 1, axis=0)
```

```python
import jax
import jax.numpy as jnp
from jax import lax
from jax.sharding import PartitionSpec as P


def passed_along(value, axis, steps):
    count = lax.axis_size(axis)
    pairs = [(source, (source + steps) % count) for source in range(count)]
    return lax.ppermute(value, axis, pairs)


def admission(chosen, language, capacity, experts):
    lang_count = capacity.shape[0]
    hit_table = jnp.sum(
        (chosen[:, :, None] == jnp.arange(experts, dtype=jnp.int32)[None, None, :]).astype(
            jnp.int32
        ),
        axis=1,
    )
    lang_hot = (language[:, None] == jnp.arange(lang_count, dtype=jnp.int32)[None, :]).astype(
        jnp.int32
    )
    lang_hits = lang_hot[:, :, None] * hit_table[:, None, :]
    before = jnp.cumsum(lang_hits, axis=0) - lang_hits
    place_rank = jnp.sum(before * lang_hot[:, :, None], axis=1)
    allowance = jnp.sum(lang_hot[:, :, None] * capacity[None, :, :], axis=1)
    admitted = hit_table * (place_rank < allowance).astype(jnp.int32)
    return (hit_table, admitted)


def slot_sources(markers, slot_table, slot_depth):
    tok_rows = markers.shape[0]
    selected = markers[:, :, None] * (
        slot_table[:, :, None] == jnp.arange(slot_depth, dtype=jnp.int32)[None, None, :]
    ).astype(jnp.int32)
    positions = jnp.arange(tok_rows, dtype=jnp.int32)[:, None, None]
    source = jnp.sum(selected * positions, axis=0)
    filled = jnp.sum(selected, axis=0)
    return jnp.where(filled > 0, source, tok_rows)


def local(tokens, expert_ids, route_weight, language, capacity, spill_table, w_gate, w_up, w_down):
    experts = lax.axis_size("expert")
    reps = lax.axis_size("rep")
    chosen = expert_ids[0]
    spill_row = spill_table[0]
    tok_rows, top_count = chosen.shape
    slot_depth = min(tok_rows, max(2, 5 * tok_rows * top_count // (4 * experts)))
    expert_iota = jnp.arange(experts, dtype=jnp.int32)
    hit_table, admitted = admission(chosen, language[0], capacity, experts)
    spilled = hit_table - admitted
    main_slot = jnp.cumsum(admitted, axis=0) - admitted
    spill_slot = jnp.cumsum(spilled, axis=0) - spilled
    spill_move = (spill_row[:, None] == expert_iota[None, :]).astype(jnp.int32)
    spill_marks = jnp.sum(spilled[:, :, None] * spill_move[None, :, :], axis=1)
    spill_places = jnp.sum((spill_slot * spilled)[:, :, None] * spill_move[None, :, :], axis=1)
    rows_local = tokens[0]
    feat_width = rows_local.shape[1]
    with_blank = jnp.concatenate(
        [rows_local, jnp.zeros((1, feat_width), rows_local.dtype)], axis=0
    )
    main_source = slot_sources(admitted, main_slot, slot_depth)
    spill_source = slot_sources(spill_marks, spill_places, slot_depth)
    sources = jnp.concatenate([main_source, spill_source], axis=1)
    outgoing = jnp.take(with_blank, sources, axis=0)
    arrived = lax.all_to_all(outgoing, "expert", split_axis=0, concat_axis=0, tiled=True)
    flattened = arrived.reshape(-1, feat_width)
    all_feats = lax.all_gather(flattened, "rep", axis=0)
    gate_w = w_gate[0, 0].reshape(reps, feat_width, -1)
    up_w = w_up[0, 0].reshape(reps, feat_width, -1)
    dims = (((0, 2), (0, 1)), ((), ()))
    gate_proj = lax.dot_general(all_feats, gate_w, dims, preferred_element_type=jnp.float32)
    up_proj = lax.dot_general(all_feats, up_w, dims, preferred_element_type=jnp.float32)
    activated = (jax.nn.silu(gate_proj) * up_proj).astype(jnp.bfloat16)
    all_act = lax.all_gather(activated, "rep", axis=0)
    down_w = w_down[0, 0].reshape(reps, activated.shape[1], -1)
    produced = lax.dot_general(all_act, down_w, dims, preferred_element_type=jnp.float32)
    out_width = down_w.shape[2]
    produced = produced.astype(jnp.bfloat16).reshape(experts, 2 * slot_depth, out_width)
    returned = lax.all_to_all(produced, "expert", split_axis=0, concat_axis=0, tiled=True)
    id_match = (chosen[:, :, None] == expert_iota[None, None, :]).astype(jnp.int32)
    row_kept = jnp.sum(id_match * admitted[:, None, :], axis=2)
    row_main = jnp.sum(id_match * main_slot[:, None, :], axis=2)
    row_spill = jnp.sum(id_match * spill_slot[:, None, :], axis=2)
    row_other = jnp.sum(id_match * spill_row[None, None, :], axis=2)
    target = jnp.where(row_kept > 0, chosen, row_other)
    slot_pick = jnp.where(row_kept > 0, row_main, slot_depth + row_spill)
    row_index = target * (2 * slot_depth) + slot_pick
    picked = jnp.take(returned.reshape(-1, out_width), row_index.reshape(-1), axis=0).reshape(
        tok_rows, top_count, out_width
    )
    combined = jnp.sum(route_weight[0][:, :, None] * picked.astype(jnp.float32), axis=1).astype(
        jnp.bfloat16
    )
    forwarded = passed_along(combined, "section", 1)
    return forwarded[None]


def solution(mesh):
    in_specs = (
        P("section", "expert", "rep"),
        P("section", "expert", None),
        P("section", "expert", None),
        P("section", "expert"),
        P(),
        P("section", None),
        P("section", "expert", None, "rep"),
        P("section", "expert", None, "rep"),
        P("section", "expert", None, "rep"),
    )
    out_specs = P("section", "expert", "rep")
    return jax.shard_map(local, mesh=mesh, in_specs=in_specs, out_specs=out_specs, check_vma=False)
```

```python
import jax
import jax.numpy as jnp
from jax import lax
from jax.sharding import PartitionSpec as P


def passed_along(value, axis, steps):
    count = lax.axis_size(axis)
    pairs = [(source, (source + steps) % count) for source in range(count)]
    return lax.ppermute(value, axis, pairs)


def gathered(value, axis):
    count = lax.axis_size(axis)
    pieces = [value]
    for shift in range(1, count):
        pairs = [(source, (source + shift) % count) for source in range(count)]
        pieces.append(lax.ppermute(value, axis, pairs))
    return jnp.stack(pieces)


def arrival_order(weight, axis):
    count = lax.axis_size(axis)
    me = lax.axis_index(axis)
    origin = (me - jnp.arange(count, dtype=jnp.int32)) % count
    return jnp.take(weight, origin, axis=0)


def admission(chosen, language, capacity, experts):
    lang_count = capacity.shape[0]
    hit_table = jnp.sum(
        (chosen[:, :, None] == jnp.arange(experts, dtype=jnp.int32)[None, None, :]).astype(
            jnp.int32
        ),
        axis=1,
    )
    lang_hot = (language[:, None] == jnp.arange(lang_count, dtype=jnp.int32)[None, :]).astype(
        jnp.int32
    )
    lang_hits = lang_hot[:, :, None] * hit_table[:, None, :]
    before = jnp.cumsum(lang_hits, axis=0) - lang_hits
    place_rank = jnp.sum(before * lang_hot[:, :, None], axis=1)
    allowance = jnp.sum(lang_hot[:, :, None] * capacity[None, :, :], axis=1)
    admitted = hit_table * (place_rank < allowance).astype(jnp.int32)
    return (hit_table, admitted)


def slot_sources(markers, slot_table, slot_depth):
    tok_rows = markers.shape[0]
    selected = markers[:, :, None] * (
        slot_table[:, :, None] == jnp.arange(slot_depth, dtype=jnp.int32)[None, None, :]
    ).astype(jnp.int32)
    positions = jnp.arange(tok_rows, dtype=jnp.int32)[:, None, None]
    source = jnp.sum(selected * positions, axis=0)
    filled = jnp.sum(selected, axis=0)
    return jnp.where(filled > 0, source, tok_rows)


def local(tokens, expert_ids, route_weight, language, capacity, spill_table, w_gate, w_up, w_down):
    experts = lax.axis_size("expert")
    reps = lax.axis_size("rep")
    chosen = expert_ids[0]
    spill_row = spill_table[0]
    tok_rows, top_count = chosen.shape
    slot_depth = min(tok_rows, max(2, 5 * tok_rows * top_count // (4 * experts)))
    expert_iota = jnp.arange(experts, dtype=jnp.int32)
    hit_table, admitted = admission(chosen, language[0], capacity, experts)
    spilled = hit_table - admitted
    main_slot = jnp.cumsum(admitted, axis=0) - admitted
    spill_slot = jnp.cumsum(spilled, axis=0) - spilled
    spill_move = (spill_row[:, None] == expert_iota[None, :]).astype(jnp.int32)
    spill_marks = jnp.sum(spilled[:, :, None] * spill_move[None, :, :], axis=1)
    spill_places = jnp.sum((spill_slot * spilled)[:, :, None] * spill_move[None, :, :], axis=1)
    rows_local = tokens[0]
    feat_width = rows_local.shape[1]
    with_blank = jnp.concatenate(
        [rows_local, jnp.zeros((1, feat_width), rows_local.dtype)], axis=0
    )
    main_source = slot_sources(admitted, main_slot, slot_depth)
    spill_source = slot_sources(spill_marks, spill_places, slot_depth)
    sources = jnp.concatenate([main_source, spill_source], axis=1)
    outgoing = jnp.take(with_blank, sources, axis=0)
    arrived = lax.all_to_all(outgoing, "expert", split_axis=0, concat_axis=0, tiled=True)
    flattened = arrived.reshape(-1, feat_width)
    all_feats = gathered(flattened, "rep")
    gate_w = arrival_order(w_gate[0, 0].reshape(reps, feat_width, -1), "rep")
    up_w = arrival_order(w_up[0, 0].reshape(reps, feat_width, -1), "rep")
    dims = (((0, 2), (0, 1)), ((), ()))
    gate_proj = lax.dot_general(all_feats, gate_w, dims, preferred_element_type=jnp.float32)
    up_proj = lax.dot_general(all_feats, up_w, dims, preferred_element_type=jnp.float32)
    activated = (jax.nn.silu(gate_proj) * up_proj).astype(jnp.bfloat16)
    all_act = gathered(activated, "rep")
    down_w = arrival_order(w_down[0, 0].reshape(reps, activated.shape[1], -1), "rep")
    produced = lax.dot_general(all_act, down_w, dims, preferred_element_type=jnp.float32)
    out_width = down_w.shape[2]
    produced = produced.astype(jnp.bfloat16).reshape(experts, 2 * slot_depth, out_width)
    returned = lax.all_to_all(produced, "expert", split_axis=0, concat_axis=0, tiled=True)
    id_match = (chosen[:, :, None] == expert_iota[None, None, :]).astype(jnp.int32)
    row_kept = jnp.sum(id_match * admitted[:, None, :], axis=2)
    row_main = jnp.sum(id_match * main_slot[:, None, :], axis=2)
    row_spill = jnp.sum(id_match * spill_slot[:, None, :], axis=2)
    row_other = jnp.sum(id_match * spill_row[None, None, :], axis=2)
    target = jnp.where(row_kept > 0, chosen, row_other)
    slot_pick = jnp.where(row_kept > 0, row_main, slot_depth + row_spill)
    row_index = target * (2 * slot_depth) + slot_pick
    picked = jnp.take(returned.reshape(-1, out_width), row_index.reshape(-1), axis=0).reshape(
        tok_rows, top_count, out_width
    )
    combined = jnp.sum(route_weight[0][:, :, None] * picked.astype(jnp.float32), axis=1).astype(
        jnp.bfloat16
    )
    forwarded = passed_along(combined, "section", 1)
    return forwarded[None]


def solution(mesh):
    in_specs = (
        P("section", "expert", "rep"),
        P("section", "expert", None),
        P("section", "expert", None),
        P("section", "expert"),
        P(),
        P("section", None),
        P("section", "expert", None, "rep"),
        P("section", "expert", None, "rep"),
        P("section", "expert", None, "rep"),
    )
    out_specs = P("section", "expert", "rep")
    return jax.shard_map(local, mesh=mesh, in_specs=in_specs, out_specs=out_specs, check_vma=False)
```

```python
import jax
import jax.numpy as jnp
from jax import lax
from jax.sharding import PartitionSpec as P


def passed_along(value, axis, steps):
    count = lax.axis_size(axis)
    pairs = [(source, (source + steps) % count) for source in range(count)]
    return lax.ppermute(value, axis, pairs)


def gathered(value, axis):
    count = lax.axis_size(axis)
    pieces = [value]
    for shift in range(1, count):
        pairs = [(source, (source + shift) % count) for source in range(count)]
        pieces.append(lax.ppermute(value, axis, pairs))
    return jnp.stack(pieces)


def arrival_order(weight, axis):
    count = lax.axis_size(axis)
    me = lax.axis_index(axis)
    origin = (me - jnp.arange(count, dtype=jnp.int32)) % count
    return jnp.take(weight, origin, axis=0)


def admission(chosen, language, capacity, experts):
    lang_count = capacity.shape[0]
    hit_table = jnp.sum(
        (chosen[:, :, None] == jnp.arange(experts, dtype=jnp.int32)[None, None, :]).astype(
            jnp.int32
        ),
        axis=1,
    )
    lang_hot = (language[:, None] == jnp.arange(lang_count, dtype=jnp.int32)[None, :]).astype(
        jnp.int32
    )
    lang_hits = lang_hot[:, :, None] * hit_table[:, None, :]
    before = jnp.cumsum(lang_hits, axis=0) - lang_hits
    place_rank = jnp.sum(before * lang_hot[:, :, None], axis=1)
    allowance = jnp.sum(lang_hot[:, :, None] * capacity[None, :, :], axis=1)
    admitted = hit_table * (place_rank < allowance).astype(jnp.int32)
    return (hit_table, admitted)


def slot_sources(markers, slot_table, slot_depth):
    tok_rows = markers.shape[0]
    selected = markers[:, :, None] * (
        slot_table[:, :, None] == jnp.arange(slot_depth, dtype=jnp.int32)[None, None, :]
    ).astype(jnp.int32)
    positions = jnp.arange(tok_rows, dtype=jnp.int32)[:, None, None]
    source = jnp.sum(selected * positions, axis=0)
    filled = jnp.sum(selected, axis=0)
    return jnp.where(filled > 0, source, tok_rows)


def local(tokens, expert_ids, route_weight, language, capacity, spill_table, w_gate, w_up, w_down):
    experts = lax.axis_size("expert")
    reps = lax.axis_size("rep")
    chosen = expert_ids[0]
    spill_row = spill_table[0]
    tok_rows, top_count = chosen.shape
    slot_depth = min(tok_rows, max(2, 5 * tok_rows * top_count // (4 * experts)))
    expert_iota = jnp.arange(experts, dtype=jnp.int32)
    hit_table, admitted = admission(chosen, language[0], capacity, experts)
    spilled = hit_table - admitted
    main_slot = jnp.cumsum(admitted, axis=0) - admitted
    spill_slot = jnp.cumsum(spilled, axis=0) - spilled
    spill_move = (spill_row[:, None] == expert_iota[None, :]).astype(jnp.int32)
    spill_marks = jnp.sum(spilled[:, :, None] * spill_move[None, :, :], axis=1)
    spill_places = jnp.sum((spill_slot * spilled)[:, :, None] * spill_move[None, :, :], axis=1)
    rows_local = tokens[0]
    feat_width = rows_local.shape[1]
    with_blank = jnp.concatenate(
        [rows_local, jnp.zeros((1, feat_width), rows_local.dtype)], axis=0
    )
    main_source = slot_sources(admitted, main_slot, slot_depth)
    spill_source = slot_sources(spill_marks, spill_places, slot_depth)
    sources = jnp.concatenate([main_source, spill_source], axis=1)
    outgoing = jnp.take(with_blank, sources, axis=0)
    arrived = lax.all_to_all(outgoing, "expert", split_axis=0, concat_axis=0, tiled=True)
    flattened = arrived.reshape(-1, feat_width)
    all_feats = lax.all_gather(flattened, "rep", axis=0)
    gate_w = w_gate[0, 0].reshape(reps, feat_width, -1)
    up_w = w_up[0, 0].reshape(reps, feat_width, -1)
    dims = (((0, 2), (0, 1)), ((), ()))
    gate_proj = lax.dot_general(all_feats, gate_w, dims, preferred_element_type=jnp.float32)
    up_proj = lax.dot_general(all_feats, up_w, dims, preferred_element_type=jnp.float32)
    activated = (jax.nn.silu(gate_proj) * up_proj).astype(jnp.bfloat16)
    all_act = gathered(activated, "rep")
    down_w = arrival_order(w_down[0, 0].reshape(reps, activated.shape[1], -1), "rep")
    produced = lax.dot_general(all_act, down_w, dims, preferred_element_type=jnp.float32)
    out_width = down_w.shape[2]
    produced = produced.astype(jnp.bfloat16).reshape(experts, 2 * slot_depth, out_width)
    returned = lax.all_to_all(produced, "expert", split_axis=0, concat_axis=0, tiled=True)
    id_match = (chosen[:, :, None] == expert_iota[None, None, :]).astype(jnp.int32)
    row_kept = jnp.sum(id_match * admitted[:, None, :], axis=2)
    row_main = jnp.sum(id_match * main_slot[:, None, :], axis=2)
    row_spill = jnp.sum(id_match * spill_slot[:, None, :], axis=2)
    row_other = jnp.sum(id_match * spill_row[None, None, :], axis=2)
    target = jnp.where(row_kept > 0, chosen, row_other)
    slot_pick = jnp.where(row_kept > 0, row_main, slot_depth + row_spill)
    row_index = target * (2 * slot_depth) + slot_pick
    picked = jnp.take(returned.reshape(-1, out_width), row_index.reshape(-1), axis=0).reshape(
        tok_rows, top_count, out_width
    )
    combined = jnp.sum(route_weight[0][:, :, None] * picked.astype(jnp.float32), axis=1).astype(
        jnp.bfloat16
    )
    forwarded = passed_along(combined, "section", 1)
    return forwarded[None]


def solution(mesh):
    in_specs = (
        P("section", "expert", "rep"),
        P("section", "expert", None),
        P("section", "expert", None),
        P("section", "expert"),
        P(),
        P("section", None),
        P("section", "expert", None, "rep"),
        P("section", "expert", None, "rep"),
        P("section", "expert", None, "rep"),
    )
    out_specs = P("section", "expert", "rep")
    return jax.shard_map(local, mesh=mesh, in_specs=in_specs, out_specs=out_specs, check_vma=False)
```

```python
import jax
import jax.numpy as jnp
from jax import lax
from jax.sharding import PartitionSpec as P


def passed_along(value, axis, steps):
    count = lax.axis_size(axis)
    pairs = [(source, (source + steps) % count) for source in range(count)]
    return lax.ppermute(value, axis, pairs)


def gathered(value, axis):
    count = lax.axis_size(axis)
    pieces = [value]
    for shift in range(1, count):
        pairs = [(source, (source + shift) % count) for source in range(count)]
        pieces.append(lax.ppermute(value, axis, pairs))
    return jnp.stack(pieces)


def arrival_order(weight, axis):
    count = lax.axis_size(axis)
    me = lax.axis_index(axis)
    origin = (me - jnp.arange(count, dtype=jnp.int32)) % count
    return jnp.take(weight, origin, axis=0)


def admission(chosen, language, capacity, experts):
    lang_count = capacity.shape[0]
    hit_table = jnp.sum(
        (chosen[:, :, None] == jnp.arange(experts, dtype=jnp.int32)[None, None, :]).astype(
            jnp.int32
        ),
        axis=1,
    )
    lang_hot = (language[:, None] == jnp.arange(lang_count, dtype=jnp.int32)[None, :]).astype(
        jnp.int32
    )
    lang_hits = lang_hot[:, :, None] * hit_table[:, None, :]
    before = jnp.cumsum(lang_hits, axis=0) - lang_hits
    place_rank = jnp.sum(before * lang_hot[:, :, None], axis=1)
    allowance = jnp.sum(lang_hot[:, :, None] * capacity[None, :, :], axis=1)
    admitted = hit_table * (place_rank < allowance).astype(jnp.int32)
    return (hit_table, admitted)


def slot_sources(markers, slot_table, slot_depth):
    tok_rows = markers.shape[0]
    selected = markers[:, :, None] * (
        slot_table[:, :, None] == jnp.arange(slot_depth, dtype=jnp.int32)[None, None, :]
    ).astype(jnp.int32)
    positions = jnp.arange(tok_rows, dtype=jnp.int32)[:, None, None]
    source = jnp.sum(selected * positions, axis=0)
    filled = jnp.sum(selected, axis=0)
    return jnp.where(filled > 0, source, tok_rows)


def local(tokens, expert_ids, route_weight, language, capacity, spill_table, w_gate, w_up, w_down):
    experts = lax.axis_size("expert")
    reps = lax.axis_size("rep")
    chosen = expert_ids[0]
    spill_row = spill_table[0]
    tok_rows, top_count = chosen.shape
    slot_depth = min(tok_rows, max(2, 5 * tok_rows * top_count // (4 * experts)))
    expert_iota = jnp.arange(experts, dtype=jnp.int32)
    hit_table, admitted = admission(chosen, language[0], capacity, experts)
    spilled = hit_table - admitted
    main_slot = jnp.cumsum(admitted, axis=0) - admitted
    spill_slot = jnp.cumsum(spilled, axis=0) - spilled
    spill_move = (spill_row[:, None] == expert_iota[None, :]).astype(jnp.int32)
    spill_marks = jnp.sum(spilled[:, :, None] * spill_move[None, :, :], axis=1)
    spill_places = jnp.sum((spill_slot * spilled)[:, :, None] * spill_move[None, :, :], axis=1)
    rows_local = tokens[0]
    feat_width = rows_local.shape[1]
    with_blank = jnp.concatenate(
        [rows_local, jnp.zeros((1, feat_width), rows_local.dtype)], axis=0
    )
    main_source = slot_sources(admitted, main_slot, slot_depth)
    spill_source = slot_sources(spill_marks, spill_places, slot_depth)
    gate_w = w_gate[0, 0].reshape(reps, feat_width, -1)
    up_w = w_up[0, 0].reshape(reps, feat_width, -1)
    down_local = w_down[0, 0]
    dims = (((0, 2), (0, 1)), ((), ()))

    def stream(sources):
        outgoing = jnp.take(with_blank, sources, axis=0)
        arrived = lax.all_to_all(outgoing, "expert", split_axis=0, concat_axis=0, tiled=True)
        flattened = arrived.reshape(-1, feat_width)
        all_feats = lax.all_gather(flattened, "rep", axis=0)
        gate_proj = lax.dot_general(all_feats, gate_w, dims, preferred_element_type=jnp.float32)
        up_proj = lax.dot_general(all_feats, up_w, dims, preferred_element_type=jnp.float32)
        activated = (jax.nn.silu(gate_proj) * up_proj).astype(jnp.bfloat16)
        all_act = gathered(activated, "rep")
        down_w = arrival_order(down_local.reshape(reps, activated.shape[1], -1), "rep")
        produced = lax.dot_general(all_act, down_w, dims, preferred_element_type=jnp.float32)
        produced = produced.astype(jnp.bfloat16).reshape(experts, slot_depth, -1)
        return lax.all_to_all(produced, "expert", split_axis=0, concat_axis=0, tiled=True)

    returned = jnp.concatenate([stream(main_source), stream(spill_source)], axis=1)
    out_width = returned.shape[2]
    id_match = (chosen[:, :, None] == expert_iota[None, None, :]).astype(jnp.int32)
    row_kept = jnp.sum(id_match * admitted[:, None, :], axis=2)
    row_main = jnp.sum(id_match * main_slot[:, None, :], axis=2)
    row_spill = jnp.sum(id_match * spill_slot[:, None, :], axis=2)
    row_other = jnp.sum(id_match * spill_row[None, None, :], axis=2)
    target = jnp.where(row_kept > 0, chosen, row_other)
    slot_pick = jnp.where(row_kept > 0, row_main, slot_depth + row_spill)
    row_index = target * (2 * slot_depth) + slot_pick
    picked = jnp.take(returned.reshape(-1, out_width), row_index.reshape(-1), axis=0).reshape(
        tok_rows, top_count, out_width
    )
    combined = jnp.sum(route_weight[0][:, :, None] * picked.astype(jnp.float32), axis=1).astype(
        jnp.bfloat16
    )
    forwarded = passed_along(combined, "section", 1)
    return forwarded[None]


def solution(mesh):
    in_specs = (
        P("section", "expert", "rep"),
        P("section", "expert", None),
        P("section", "expert", None),
        P("section", "expert"),
        P(),
        P("section", None),
        P("section", "expert", None, "rep"),
        P("section", "expert", None, "rep"),
        P("section", "expert", None, "rep"),
    )
    out_specs = P("section", "expert", "rep")
    return jax.shard_map(local, mesh=mesh, in_specs=in_specs, out_specs=out_specs, check_vma=False)
```

```python
import jax
import jax.numpy as jnp
from jax import lax
from jax.sharding import PartitionSpec as P


def passed_along(value, axis, steps):
    count = lax.axis_size(axis)
    pairs = [(source, (source + steps) % count) for source in range(count)]
    return lax.ppermute(value, axis, pairs)


def gathered(value, axis):
    count = lax.axis_size(axis)
    pieces = [value]
    for shift in range(1, count):
        pairs = [(source, (source + shift) % count) for source in range(count)]
        pieces.append(lax.ppermute(value, axis, pairs))
    return jnp.stack(pieces)


def arrival_order(weight, axis):
    count = lax.axis_size(axis)
    me = lax.axis_index(axis)
    origin = (me - jnp.arange(count, dtype=jnp.int32)) % count
    return jnp.take(weight, origin, axis=0)


def admission(chosen, language, capacity, experts):
    lang_count = capacity.shape[0]
    hit_table = jnp.sum(
        (chosen[:, :, None] == jnp.arange(experts, dtype=jnp.int32)[None, None, :]).astype(
            jnp.int32
        ),
        axis=1,
    )
    lang_hot = (language[:, None] == jnp.arange(lang_count, dtype=jnp.int32)[None, :]).astype(
        jnp.int32
    )
    lang_hits = lang_hot[:, :, None] * hit_table[:, None, :]
    before = jnp.cumsum(lang_hits, axis=0) - lang_hits
    place_rank = jnp.sum(before * lang_hot[:, :, None], axis=1)
    allowance = jnp.sum(lang_hot[:, :, None] * capacity[None, :, :], axis=1)
    admitted = hit_table * (place_rank < allowance).astype(jnp.int32)
    return (hit_table, admitted)


def slot_sources(markers, slot_table, slot_depth):
    tok_rows = markers.shape[0]
    selected = markers[:, :, None] * (
        slot_table[:, :, None] == jnp.arange(slot_depth, dtype=jnp.int32)[None, None, :]
    ).astype(jnp.int32)
    positions = jnp.arange(tok_rows, dtype=jnp.int32)[:, None, None]
    source = jnp.sum(selected * positions, axis=0)
    filled = jnp.sum(selected, axis=0)
    return jnp.where(filled > 0, source, tok_rows)


def local(tokens, expert_ids, route_weight, language, capacity, spill_table, w_gate, w_up, w_down):
    experts = lax.axis_size("expert")
    reps = lax.axis_size("rep")
    chosen = expert_ids[0]
    spill_row = spill_table[0]
    tok_rows, top_count = chosen.shape
    slot_depth = min(tok_rows, max(2, 5 * tok_rows * top_count // (4 * experts)))
    expert_iota = jnp.arange(experts, dtype=jnp.int32)
    hit_table, admitted = admission(chosen, language[0], capacity, experts)
    spilled = hit_table - admitted
    main_slot = jnp.cumsum(admitted, axis=0) - admitted
    spill_slot = jnp.cumsum(spilled, axis=0) - spilled
    spill_move = (spill_row[:, None] == expert_iota[None, :]).astype(jnp.int32)
    spill_marks = jnp.sum(spilled[:, :, None] * spill_move[None, :, :], axis=1)
    spill_places = jnp.sum((spill_slot * spilled)[:, :, None] * spill_move[None, :, :], axis=1)
    rows_local = tokens[0]
    feat_width = rows_local.shape[1]
    routing = jnp.concatenate([chosen, language[0][:, None]], axis=1)
    all_routing = lax.all_gather(routing, "expert", axis=0)
    all_rows = lax.all_gather(rows_local, "expert", axis=0)
    me = lax.axis_index("expert")
    mine = (expert_iota == me).astype(jnp.int32)
    spill_mine = (spill_row == me).astype(jnp.int32)

    def block_pick(block_routing):
        block_hits, block_admitted = admission(
            block_routing[:, :top_count], block_routing[:, top_count], capacity, experts
        )
        block_spilled = block_hits - block_admitted
        marks = jnp.stack(
            [block_admitted @ mine, block_spilled @ spill_mine], axis=1
        )
        places = jnp.cumsum(marks, axis=0) - marks
        sources = slot_sources(marks, places, slot_depth).reshape(-1)
        return (sources[:, None] == jnp.arange(tok_rows, dtype=jnp.int32)[None, :]).astype(
            rows_local.dtype
        )

    picks = jax.vmap(block_pick)(all_routing)
    arrived = jnp.einsum(
        "bjt,btf->bjf", picks, all_rows, preferred_element_type=jnp.float32
    ).astype(rows_local.dtype)
    flattened = arrived.reshape(-1, feat_width)
    all_feats = lax.all_gather(flattened, "rep", axis=0)
    gate_w = w_gate[0, 0].reshape(reps, feat_width, -1)
    up_w = w_up[0, 0].reshape(reps, feat_width, -1)
    dims = (((0, 2), (0, 1)), ((), ()))
    gate_proj = lax.dot_general(all_feats, gate_w, dims, preferred_element_type=jnp.float32)
    up_proj = lax.dot_general(all_feats, up_w, dims, preferred_element_type=jnp.float32)
    activated = (jax.nn.silu(gate_proj) * up_proj).astype(jnp.bfloat16)
    all_act = gathered(activated, "rep")
    down_w = arrival_order(w_down[0, 0].reshape(reps, activated.shape[1], -1), "rep")
    produced = lax.dot_general(all_act, down_w, dims, preferred_element_type=jnp.float32)
    out_width = down_w.shape[2]
    produced = produced.astype(jnp.bfloat16).reshape(experts, 2 * slot_depth, out_width)
    returned = lax.all_to_all(produced, "expert", split_axis=0, concat_axis=0, tiled=True)
    id_match = (chosen[:, :, None] == expert_iota[None, None, :]).astype(jnp.int32)
    row_kept = jnp.sum(id_match * admitted[:, None, :], axis=2)
    row_main = jnp.sum(id_match * main_slot[:, None, :], axis=2)
    row_spill = jnp.sum(id_match * spill_slot[:, None, :], axis=2)
    row_other = jnp.sum(id_match * spill_row[None, None, :], axis=2)
    target = jnp.where(row_kept > 0, chosen, row_other)
    slot_pick = jnp.where(row_kept > 0, row_main, slot_depth + row_spill)
    row_index = target * (2 * slot_depth) + slot_pick
    picked = jnp.take(returned.reshape(-1, out_width), row_index.reshape(-1), axis=0).reshape(
        tok_rows, top_count, out_width
    )
    combined = jnp.sum(route_weight[0][:, :, None] * picked.astype(jnp.float32), axis=1).astype(
        jnp.bfloat16
    )
    forwarded = passed_along(combined, "section", 1)
    return forwarded[None]


def solution(mesh):
    in_specs = (
        P("section", "expert", "rep"),
        P("section", "expert", None),
        P("section", "expert", None),
        P("section", "expert"),
        P(),
        P("section", None),
        P("section", "expert", None, "rep"),
        P("section", "expert", None, "rep"),
        P("section", "expert", None, "rep"),
    )
    out_specs = P("section", "expert", "rep")
    return jax.shard_map(local, mesh=mesh, in_specs=in_specs, out_specs=out_specs, check_vma=False)
```

```python
import jax
import jax.numpy as jnp
from jax import lax
from jax.sharding import PartitionSpec as P


def passed_along(value, axis, steps):
    count = lax.axis_size(axis)
    pairs = [(source, (source + steps) % count) for source in range(count)]
    return lax.ppermute(value, axis, pairs)


def gathered(value, axis):
    count = lax.axis_size(axis)
    pieces = [value]
    for shift in range(1, count):
        pairs = [(source, (source + shift) % count) for source in range(count)]
        pieces.append(lax.ppermute(value, axis, pairs))
    return pieces


def arrival_order(weight, axis):
    count = lax.axis_size(axis)
    me = lax.axis_index(axis)
    origin = (me - jnp.arange(count, dtype=jnp.int32)) % count
    return jnp.take(weight, origin, axis=0)


def admission(chosen, language, capacity, experts):
    lang_count = capacity.shape[0]
    hit_table = jnp.sum(
        (chosen[:, :, None] == jnp.arange(experts, dtype=jnp.int32)[None, None, :]).astype(
            jnp.int32
        ),
        axis=1,
    )
    lang_hot = (language[:, None] == jnp.arange(lang_count, dtype=jnp.int32)[None, :]).astype(
        jnp.int32
    )
    lang_hits = lang_hot[:, :, None] * hit_table[:, None, :]
    before = jnp.cumsum(lang_hits, axis=0) - lang_hits
    place_rank = jnp.sum(before * lang_hot[:, :, None], axis=1)
    allowance = jnp.sum(lang_hot[:, :, None] * capacity[None, :, :], axis=1)
    admitted = hit_table * (place_rank < allowance).astype(jnp.int32)
    return (hit_table, admitted)


def slot_sources(markers, slot_table, slot_depth):
    tok_rows = markers.shape[0]
    selected = markers[:, :, None] * (
        slot_table[:, :, None] == jnp.arange(slot_depth, dtype=jnp.int32)[None, None, :]
    ).astype(jnp.int32)
    positions = jnp.arange(tok_rows, dtype=jnp.int32)[:, None, None]
    source = jnp.sum(selected * positions, axis=0)
    filled = jnp.sum(selected, axis=0)
    return jnp.where(filled > 0, source, tok_rows)


def local(tokens, expert_ids, route_weight, language, capacity, spill_table, w_gate, w_up, w_down):
    experts = lax.axis_size("expert")
    reps = lax.axis_size("rep")
    chosen = expert_ids[0]
    spill_row = spill_table[0]
    tok_rows, top_count = chosen.shape
    slot_depth = min(tok_rows, max(2, 5 * tok_rows * top_count // (4 * experts)))
    expert_iota = jnp.arange(experts, dtype=jnp.int32)
    hit_table, admitted = admission(chosen, language[0], capacity, experts)
    spilled = hit_table - admitted
    main_slot = jnp.cumsum(admitted, axis=0) - admitted
    spill_slot = jnp.cumsum(spilled, axis=0) - spilled
    spill_move = (spill_row[:, None] == expert_iota[None, :]).astype(jnp.int32)
    spill_marks = jnp.sum(spilled[:, :, None] * spill_move[None, :, :], axis=1)
    spill_places = jnp.sum((spill_slot * spilled)[:, :, None] * spill_move[None, :, :], axis=1)
    rows_local = tokens[0]
    feat_width = rows_local.shape[1]
    with_blank = jnp.concatenate(
        [rows_local, jnp.zeros((1, feat_width), rows_local.dtype)], axis=0
    )
    main_source = slot_sources(admitted, main_slot, slot_depth)
    spill_source = slot_sources(spill_marks, spill_places, slot_depth)
    sources = jnp.concatenate([main_source, spill_source], axis=1)
    outgoing = jnp.take(with_blank, sources, axis=0)
    arrived = lax.all_to_all(outgoing, "expert", split_axis=0, concat_axis=0, tiled=True)
    flattened = arrived.reshape(-1, feat_width)
    all_feats = lax.all_gather(flattened, "rep", axis=0)
    gate_w = w_gate[0, 0].reshape(reps, feat_width, -1)
    up_w = w_up[0, 0].reshape(reps, feat_width, -1)
    dims = (((0, 2), (0, 1)), ((), ()))
    gate_proj = lax.dot_general(all_feats, gate_w, dims, preferred_element_type=jnp.float32)
    up_proj = lax.dot_general(all_feats, up_w, dims, preferred_element_type=jnp.float32)
    activated = (jax.nn.silu(gate_proj) * up_proj).astype(jnp.bfloat16)
    all_act = gathered(activated, "rep")
    down_w = arrival_order(w_down[0, 0].reshape(reps, activated.shape[1], -1), "rep")
    produced = jnp.dot(all_act[0], down_w[0], preferred_element_type=jnp.float32)
    for shift in range(1, reps):
        produced = produced + jnp.dot(
            all_act[shift], down_w[shift], preferred_element_type=jnp.float32
        )
    out_width = down_w.shape[2]
    produced = produced.astype(jnp.bfloat16).reshape(experts, 2 * slot_depth, out_width)
    returned = lax.all_to_all(produced, "expert", split_axis=0, concat_axis=0, tiled=True)
    id_match = (chosen[:, :, None] == expert_iota[None, None, :]).astype(jnp.int32)
    row_kept = jnp.sum(id_match * admitted[:, None, :], axis=2)
    row_main = jnp.sum(id_match * main_slot[:, None, :], axis=2)
    row_spill = jnp.sum(id_match * spill_slot[:, None, :], axis=2)
    row_other = jnp.sum(id_match * spill_row[None, None, :], axis=2)
    target = jnp.where(row_kept > 0, chosen, row_other)
    slot_pick = jnp.where(row_kept > 0, row_main, slot_depth + row_spill)
    row_index = target * (2 * slot_depth) + slot_pick
    picked = jnp.take(returned.reshape(-1, out_width), row_index.reshape(-1), axis=0).reshape(
        tok_rows, top_count, out_width
    )
    combined = jnp.sum(route_weight[0][:, :, None] * picked.astype(jnp.float32), axis=1).astype(
        jnp.bfloat16
    )
    forwarded = passed_along(combined, "section", 1)
    return forwarded[None]


def solution(mesh):
    in_specs = (
        P("section", "expert", "rep"),
        P("section", "expert", None),
        P("section", "expert", None),
        P("section", "expert"),
        P(),
        P("section", None),
        P("section", "expert", None, "rep"),
        P("section", "expert", None, "rep"),
        P("section", "expert", None, "rep"),
    )
    out_specs = P("section", "expert", "rep")
    return jax.shard_map(local, mesh=mesh, in_specs=in_specs, out_specs=out_specs, check_vma=False)
```

```python
import jax
import jax.numpy as jnp
from jax import lax
from jax.sharding import PartitionSpec as P


def passed_along(value, axis, steps):
    count = lax.axis_size(axis)
    pairs = [(source, (source + steps) % count) for source in range(count)]
    return lax.ppermute(value, axis, pairs)


def gathered(value, axis):
    count = lax.axis_size(axis)
    pieces = [value]
    for shift in range(1, count):
        pairs = [(source, (source + shift) % count) for source in range(count)]
        pieces.append(lax.ppermute(value, axis, pairs))
    return pieces


def paired_gather(value, axis):
    count = lax.axis_size(axis)
    me = lax.axis_index(axis)
    partner = lax.ppermute(value, axis, [(source, source ^ 1) for source in range(count)])
    pair = jnp.stack([value, partner])
    pieces = [value, partner]
    origins = [me, me ^ 1]
    for shift in range(2, count, 2):
        pairs = [(source, (source + shift) % count) for source in range(count)]
        moved = lax.ppermute(pair, axis, pairs)
        origin = (me - shift) % count
        pieces.extend([moved[0], moved[1]])
        origins.extend([origin, origin ^ 1])
    return pieces, jnp.stack(origins)


def arrival_order(weight, axis):
    count = lax.axis_size(axis)
    me = lax.axis_index(axis)
    origin = (me - jnp.arange(count, dtype=jnp.int32)) % count
    return jnp.take(weight, origin, axis=0)


def admission(chosen, language, capacity, experts):
    lang_count = capacity.shape[0]
    hit_table = jnp.sum(
        (chosen[:, :, None] == jnp.arange(experts, dtype=jnp.int32)[None, None, :]).astype(
            jnp.int32
        ),
        axis=1,
    )
    lang_hot = (language[:, None] == jnp.arange(lang_count, dtype=jnp.int32)[None, :]).astype(
        jnp.int32
    )
    lang_hits = lang_hot[:, :, None] * hit_table[:, None, :]
    before = jnp.cumsum(lang_hits, axis=0) - lang_hits
    place_rank = jnp.sum(before * lang_hot[:, :, None], axis=1)
    allowance = jnp.sum(lang_hot[:, :, None] * capacity[None, :, :], axis=1)
    admitted = hit_table * (place_rank < allowance).astype(jnp.int32)
    return (hit_table, admitted)


def slot_sources(markers, slot_table, slot_depth):
    tok_rows = markers.shape[0]
    selected = markers[:, :, None] * (
        slot_table[:, :, None] == jnp.arange(slot_depth, dtype=jnp.int32)[None, None, :]
    ).astype(jnp.int32)
    positions = jnp.arange(tok_rows, dtype=jnp.int32)[:, None, None]
    source = jnp.sum(selected * positions, axis=0)
    filled = jnp.sum(selected, axis=0)
    return jnp.where(filled > 0, source, tok_rows)


def local(tokens, expert_ids, route_weight, language, capacity, spill_table, w_gate, w_up, w_down):
    experts = lax.axis_size("expert")
    reps = lax.axis_size("rep")
    chosen = expert_ids[0]
    spill_row = spill_table[0]
    tok_rows, top_count = chosen.shape
    slot_depth = min(tok_rows, max(2, 5 * tok_rows * top_count // (4 * experts)))
    expert_iota = jnp.arange(experts, dtype=jnp.int32)
    hit_table, admitted = admission(chosen, language[0], capacity, experts)
    spilled = hit_table - admitted
    main_slot = jnp.cumsum(admitted, axis=0) - admitted
    spill_slot = jnp.cumsum(spilled, axis=0) - spilled
    spill_move = (spill_row[:, None] == expert_iota[None, :]).astype(jnp.int32)
    spill_marks = jnp.sum(spilled[:, :, None] * spill_move[None, :, :], axis=1)
    spill_places = jnp.sum((spill_slot * spilled)[:, :, None] * spill_move[None, :, :], axis=1)
    rows_local = tokens[0]
    feat_width = rows_local.shape[1]
    main_source = slot_sources(admitted, main_slot, slot_depth)
    spill_source = slot_sources(spill_marks, spill_places, slot_depth)
    sources = jnp.concatenate([main_source, spill_source], axis=1)
    picks = (sources[:, :, None] == jnp.arange(tok_rows, dtype=jnp.int32)[None, None, :]).astype(
        rows_local.dtype
    )
    outgoing = jnp.einsum(
        "xjt,tf->xjf", picks, rows_local, preferred_element_type=jnp.float32
    ).astype(rows_local.dtype)
    arrived = lax.all_to_all(outgoing, "expert", split_axis=0, concat_axis=0, tiled=True)
    flattened = arrived.reshape(-1, feat_width)
    all_feats = lax.all_gather(flattened, "rep", axis=0)
    gate_w = w_gate[0, 0].reshape(reps, feat_width, -1)
    up_w = w_up[0, 0].reshape(reps, feat_width, -1)
    dims = (((0, 2), (0, 1)), ((), ()))
    gate_proj = lax.dot_general(all_feats, gate_w, dims, preferred_element_type=jnp.float32)
    up_proj = lax.dot_general(all_feats, up_w, dims, preferred_element_type=jnp.float32)
    activated = (jax.nn.silu(gate_proj) * up_proj).astype(jnp.bfloat16)
    all_act, act_origins = paired_gather(activated, "rep")
    down_w = jnp.take(w_down[0, 0].reshape(reps, activated.shape[1], -1), act_origins, axis=0)
    produced = jnp.dot(all_act[0], down_w[0], preferred_element_type=jnp.float32)
    for shift in range(1, reps):
        produced = produced + jnp.dot(
            all_act[shift], down_w[shift], preferred_element_type=jnp.float32
        )
    out_width = down_w.shape[2]
    produced = produced.astype(jnp.bfloat16).reshape(experts, 2 * slot_depth, out_width)
    returned = lax.all_to_all(produced, "expert", split_axis=0, concat_axis=0, tiled=True)
    id_match = (chosen[:, :, None] == expert_iota[None, None, :]).astype(jnp.int32)
    row_kept = jnp.sum(id_match * admitted[:, None, :], axis=2)
    row_main = jnp.sum(id_match * main_slot[:, None, :], axis=2)
    row_spill = jnp.sum(id_match * spill_slot[:, None, :], axis=2)
    row_other = jnp.sum(id_match * spill_row[None, None, :], axis=2)
    target = jnp.where(row_kept > 0, chosen, row_other)
    slot_pick = jnp.where(row_kept > 0, row_main, slot_depth + row_spill)
    row_index = target * (2 * slot_depth) + slot_pick
    picked = jnp.take(returned.reshape(-1, out_width), row_index.reshape(-1), axis=0).reshape(
        tok_rows, top_count, out_width
    )
    combined = jnp.sum(route_weight[0][:, :, None] * picked.astype(jnp.float32), axis=1).astype(
        jnp.bfloat16
    )
    forwarded = passed_along(combined, "section", 1)
    return forwarded[None]


def solution(mesh):
    in_specs = (
        P("section", "expert", "rep"),
        P("section", "expert", None),
        P("section", "expert", None),
        P("section", "expert"),
        P(),
        P("section", None),
        P("section", "expert", None, "rep"),
        P("section", "expert", None, "rep"),
        P("section", "expert", None, "rep"),
    )
    out_specs = P("section", "expert", "rep")
    return jax.shard_map(local, mesh=mesh, in_specs=in_specs, out_specs=out_specs, check_vma=False)
```

```python
import jax
import jax.numpy as jnp
from jax import lax
from jax.sharding import PartitionSpec as P


def passed_along(value, axis, steps):
    count = lax.axis_size(axis)
    pairs = [(source, (source + steps) % count) for source in range(count)]
    return lax.ppermute(value, axis, pairs)


def gathered(value, axis):
    count = lax.axis_size(axis)
    pieces = [value]
    for shift in range(1, count):
        pairs = [(source, (source + shift) % count) for source in range(count)]
        pieces.append(lax.ppermute(value, axis, pairs))
    return pieces


def chips_then_core(value, axis):
    count = lax.axis_size(axis)
    me = lax.axis_index(axis)
    pieces = [value]
    origins = [me]
    for shift in range(2, count, 2):
        pairs = [(source, (source + shift) % count) for source in range(count)]
        pieces.append(lax.ppermute(value, axis, pairs))
        origins.append((me - shift) % count)
    bundle = jnp.stack(pieces)
    swapped = lax.ppermute(bundle, axis, [(source, source ^ 1) for source in range(count)])
    origins = jnp.stack(origins)
    return bundle, swapped, origins, origins ^ 1


def paired_gather(value, axis):
    count = lax.axis_size(axis)
    me = lax.axis_index(axis)
    partner = lax.ppermute(value, axis, [(source, source ^ 1) for source in range(count)])
    pair = jnp.stack([value, partner])
    pieces = [value, partner]
    origins = [me, me ^ 1]
    for shift in range(2, count, 2):
        pairs = [(source, (source + shift) % count) for source in range(count)]
        moved = lax.ppermute(pair, axis, pairs)
        origin = (me - shift) % count
        pieces.extend([moved[0], moved[1]])
        origins.extend([origin, origin ^ 1])
    return pieces, jnp.stack(origins)


def arrival_order(weight, axis):
    count = lax.axis_size(axis)
    me = lax.axis_index(axis)
    origin = (me - jnp.arange(count, dtype=jnp.int32)) % count
    return jnp.take(weight, origin, axis=0)


def admission(chosen, language, capacity, experts):
    lang_count = capacity.shape[0]
    hit_table = jnp.sum(
        (chosen[:, :, None] == jnp.arange(experts, dtype=jnp.int32)[None, None, :]).astype(
            jnp.int32
        ),
        axis=1,
    )
    lang_hot = (language[:, None] == jnp.arange(lang_count, dtype=jnp.int32)[None, :]).astype(
        jnp.int32
    )
    lang_hits = lang_hot[:, :, None] * hit_table[:, None, :]
    before = jnp.cumsum(lang_hits, axis=0) - lang_hits
    place_rank = jnp.sum(before * lang_hot[:, :, None], axis=1)
    allowance = jnp.sum(lang_hot[:, :, None] * capacity[None, :, :], axis=1)
    admitted = hit_table * (place_rank < allowance).astype(jnp.int32)
    return (hit_table, admitted)


def slot_sources(markers, slot_table, slot_depth):
    tok_rows = markers.shape[0]
    selected = markers[:, :, None] * (
        slot_table[:, :, None] == jnp.arange(slot_depth, dtype=jnp.int32)[None, None, :]
    ).astype(jnp.int32)
    positions = jnp.arange(tok_rows, dtype=jnp.int32)[:, None, None]
    source = jnp.sum(selected * positions, axis=0)
    filled = jnp.sum(selected, axis=0)
    return jnp.where(filled > 0, source, tok_rows)


def local(tokens, expert_ids, route_weight, language, capacity, spill_table, w_gate, w_up, w_down):
    experts = lax.axis_size("expert")
    reps = lax.axis_size("rep")
    chosen = expert_ids[0]
    spill_row = spill_table[0]
    tok_rows, top_count = chosen.shape
    slot_depth = min(tok_rows, max(2, 5 * tok_rows * top_count // (4 * experts)))
    expert_iota = jnp.arange(experts, dtype=jnp.int32)
    hit_table, admitted = admission(chosen, language[0], capacity, experts)
    spilled = hit_table - admitted
    main_slot = jnp.cumsum(admitted, axis=0) - admitted
    spill_slot = jnp.cumsum(spilled, axis=0) - spilled
    spill_move = (spill_row[:, None] == expert_iota[None, :]).astype(jnp.int32)
    spill_marks = jnp.sum(spilled[:, :, None] * spill_move[None, :, :], axis=1)
    spill_places = jnp.sum((spill_slot * spilled)[:, :, None] * spill_move[None, :, :], axis=1)
    rows_local = tokens[0]
    feat_width = rows_local.shape[1]
    main_source = slot_sources(admitted, main_slot, slot_depth)
    spill_source = slot_sources(spill_marks, spill_places, slot_depth)
    sources = jnp.concatenate([main_source, spill_source], axis=1)
    picks = (sources[:, :, None] == jnp.arange(tok_rows, dtype=jnp.int32)[None, None, :]).astype(
        rows_local.dtype
    )
    outgoing = jnp.einsum(
        "xjt,tf->xjf", picks, rows_local, preferred_element_type=jnp.float32
    ).astype(rows_local.dtype)
    arrived = lax.all_to_all(outgoing, "expert", split_axis=0, concat_axis=0, tiled=True)
    flattened = arrived.reshape(-1, feat_width)
    own_feats, partner_feats, own_from, partner_from = chips_then_core(flattened, "rep")
    gate_all = w_gate[0, 0].reshape(reps, feat_width, -1)
    up_all = w_up[0, 0].reshape(reps, feat_width, -1)
    dims = (((0, 2), (0, 1)), ((), ()))

    def project(weights):
        own = lax.dot_general(
            own_feats, jnp.take(weights, own_from, axis=0), dims,
            preferred_element_type=jnp.float32,
        )
        partner = lax.dot_general(
            partner_feats, jnp.take(weights, partner_from, axis=0), dims,
            preferred_element_type=jnp.float32,
        )
        return own + partner

    gate_proj = project(gate_all)
    up_proj = project(up_all)
    activated = (jax.nn.silu(gate_proj) * up_proj).astype(jnp.bfloat16)
    own_act, partner_act, act_own_from, act_partner_from = chips_then_core(activated, "rep")
    down_all = w_down[0, 0].reshape(reps, activated.shape[1], -1)
    produced = lax.dot_general(
        own_act, jnp.take(down_all, act_own_from, axis=0), dims,
        preferred_element_type=jnp.float32,
    ) + lax.dot_general(
        partner_act, jnp.take(down_all, act_partner_from, axis=0), dims,
        preferred_element_type=jnp.float32,
    )
    down_w = down_all
    out_width = down_w.shape[2]
    produced = produced.astype(jnp.bfloat16).reshape(experts, 2 * slot_depth, out_width)
    returned = lax.all_to_all(produced, "expert", split_axis=0, concat_axis=0, tiled=True)
    id_match = (chosen[:, :, None] == expert_iota[None, None, :]).astype(jnp.int32)
    row_kept = jnp.sum(id_match * admitted[:, None, :], axis=2)
    row_main = jnp.sum(id_match * main_slot[:, None, :], axis=2)
    row_spill = jnp.sum(id_match * spill_slot[:, None, :], axis=2)
    row_other = jnp.sum(id_match * spill_row[None, None, :], axis=2)
    target = jnp.where(row_kept > 0, chosen, row_other)
    slot_pick = jnp.where(row_kept > 0, row_main, slot_depth + row_spill)
    row_index = target * (2 * slot_depth) + slot_pick
    picked = jnp.take(returned.reshape(-1, out_width), row_index.reshape(-1), axis=0).reshape(
        tok_rows, top_count, out_width
    )
    combined = jnp.sum(route_weight[0][:, :, None] * picked.astype(jnp.float32), axis=1).astype(
        jnp.bfloat16
    )
    forwarded = passed_along(combined, "section", 1)
    return forwarded[None]


def solution(mesh):
    in_specs = (
        P("section", "expert", "rep"),
        P("section", "expert", None),
        P("section", "expert", None),
        P("section", "expert"),
        P(),
        P("section", None),
        P("section", "expert", None, "rep"),
        P("section", "expert", None, "rep"),
        P("section", "expert", None, "rep"),
    )
    out_specs = P("section", "expert", "rep")
    return jax.shard_map(local, mesh=mesh, in_specs=in_specs, out_specs=out_specs, check_vma=False)
```

```python
import jax
import jax.numpy as jnp
from jax import lax
from jax.sharding import PartitionSpec as P


def passed_along(value, axis, steps):
    count = lax.axis_size(axis)
    pairs = [(source, (source + steps) % count) for source in range(count)]
    return lax.ppermute(value, axis, pairs)


def gathered(value, axis):
    count = lax.axis_size(axis)
    pieces = [value]
    for shift in range(1, count):
        pairs = [(source, (source + shift) % count) for source in range(count)]
        pieces.append(lax.ppermute(value, axis, pairs))
    return pieces


def chips_then_core(value, axis):
    count = lax.axis_size(axis)
    me = lax.axis_index(axis)
    pieces = [value]
    origins = [me]
    for shift in range(2, count, 2):
        pairs = [(source, (source + shift) % count) for source in range(count)]
        pieces.append(lax.ppermute(value, axis, pairs))
        origins.append((me - shift) % count)
    bundle = jnp.stack(pieces)
    swapped = lax.ppermute(bundle, axis, [(source, source ^ 1) for source in range(count)])
    origins = jnp.stack(origins)
    return bundle, swapped, origins, origins ^ 1


def relayed_chips_then_core(value, axis):
    count = lax.axis_size(axis)
    me = lax.axis_index(axis)
    up_pairs = [(source, (source + 2) % count) for source in range(count)]
    down_pairs = [(source, (source - 2) % count) for source in range(count)]
    from_below = lax.ppermute(value, axis, up_pairs)
    from_above = lax.ppermute(value, axis, down_pairs)
    half = value.shape[0] // 2
    far_low = lax.ppermute(from_below[:half], axis, up_pairs)
    far_high = lax.ppermute(from_above[half:], axis, down_pairs)
    far = jnp.concatenate([far_low, far_high], axis=0)
    bundle = jnp.stack([value, from_below, from_above, far])
    swapped = lax.ppermute(bundle, axis, [(source, source ^ 1) for source in range(count)])
    origins = jnp.stack([me, (me - 2) % count, (me + 2) % count, (me + 4) % count])
    return bundle, swapped, origins, origins ^ 1


def paired_gather(value, axis):
    count = lax.axis_size(axis)
    me = lax.axis_index(axis)
    partner = lax.ppermute(value, axis, [(source, source ^ 1) for source in range(count)])
    pair = jnp.stack([value, partner])
    pieces = [value, partner]
    origins = [me, me ^ 1]
    for shift in range(2, count, 2):
        pairs = [(source, (source + shift) % count) for source in range(count)]
        moved = lax.ppermute(pair, axis, pairs)
        origin = (me - shift) % count
        pieces.extend([moved[0], moved[1]])
        origins.extend([origin, origin ^ 1])
    return pieces, jnp.stack(origins)


def arrival_order(weight, axis):
    count = lax.axis_size(axis)
    me = lax.axis_index(axis)
    origin = (me - jnp.arange(count, dtype=jnp.int32)) % count
    return jnp.take(weight, origin, axis=0)


def admission(chosen, language, capacity, experts):
    lang_count = capacity.shape[0]
    hit_table = jnp.sum(
        (chosen[:, :, None] == jnp.arange(experts, dtype=jnp.int32)[None, None, :]).astype(
            jnp.int32
        ),
        axis=1,
    )
    lang_hot = (language[:, None] == jnp.arange(lang_count, dtype=jnp.int32)[None, :]).astype(
        jnp.int32
    )
    lang_hits = lang_hot[:, :, None] * hit_table[:, None, :]
    before = jnp.cumsum(lang_hits, axis=0) - lang_hits
    place_rank = jnp.sum(before * lang_hot[:, :, None], axis=1)
    allowance = jnp.sum(lang_hot[:, :, None] * capacity[None, :, :], axis=1)
    admitted = hit_table * (place_rank < allowance).astype(jnp.int32)
    return (hit_table, admitted)


def slot_sources(markers, slot_table, slot_depth):
    tok_rows = markers.shape[0]
    selected = markers[:, :, None] * (
        slot_table[:, :, None] == jnp.arange(slot_depth, dtype=jnp.int32)[None, None, :]
    ).astype(jnp.int32)
    positions = jnp.arange(tok_rows, dtype=jnp.int32)[:, None, None]
    source = jnp.sum(selected * positions, axis=0)
    filled = jnp.sum(selected, axis=0)
    return jnp.where(filled > 0, source, tok_rows)


def local(tokens, expert_ids, route_weight, language, capacity, spill_table, w_gate, w_up, w_down):
    experts = lax.axis_size("expert")
    reps = lax.axis_size("rep")
    chosen = expert_ids[0]
    spill_row = spill_table[0]
    tok_rows, top_count = chosen.shape
    slot_depth = min(tok_rows, max(2, 5 * tok_rows * top_count // (4 * experts)))
    expert_iota = jnp.arange(experts, dtype=jnp.int32)
    hit_table, admitted = admission(chosen, language[0], capacity, experts)
    spilled = hit_table - admitted
    main_slot = jnp.cumsum(admitted, axis=0) - admitted
    spill_slot = jnp.cumsum(spilled, axis=0) - spilled
    spill_move = (spill_row[:, None] == expert_iota[None, :]).astype(jnp.int32)
    spill_marks = jnp.sum(spilled[:, :, None] * spill_move[None, :, :], axis=1)
    spill_places = jnp.sum((spill_slot * spilled)[:, :, None] * spill_move[None, :, :], axis=1)
    rows_local = tokens[0]
    feat_width = rows_local.shape[1]
    main_source = slot_sources(admitted, main_slot, slot_depth)
    spill_source = slot_sources(spill_marks, spill_places, slot_depth)
    sources = jnp.concatenate([main_source, spill_source], axis=1)
    picks = (sources[:, :, None] == jnp.arange(tok_rows, dtype=jnp.int32)[None, None, :]).astype(
        rows_local.dtype
    )
    outgoing = jnp.einsum(
        "xjt,tf->xjf", picks, rows_local, preferred_element_type=jnp.float32
    ).astype(rows_local.dtype)
    arrived = lax.all_to_all(outgoing, "expert", split_axis=0, concat_axis=0, tiled=True)
    flattened = arrived.reshape(-1, feat_width)
    own_feats, partner_feats, own_from, partner_from = relayed_chips_then_core(flattened, "rep")
    gate_all = w_gate[0, 0].reshape(reps, feat_width, -1)
    up_all = w_up[0, 0].reshape(reps, feat_width, -1)
    dims = (((0, 2), (0, 1)), ((), ()))

    def project(weights):
        own = lax.dot_general(
            own_feats, jnp.take(weights, own_from, axis=0), dims,
            preferred_element_type=jnp.float32,
        )
        partner = lax.dot_general(
            partner_feats, jnp.take(weights, partner_from, axis=0), dims,
            preferred_element_type=jnp.float32,
        )
        return own + partner

    gate_proj = project(gate_all)
    up_proj = project(up_all)
    activated = (jax.nn.silu(gate_proj) * up_proj).astype(jnp.bfloat16)
    own_act, partner_act, act_own_from, act_partner_from = chips_then_core(activated, "rep")
    down_all = w_down[0, 0].reshape(reps, activated.shape[1], -1)
    produced = lax.dot_general(
        own_act, jnp.take(down_all, act_own_from, axis=0), dims,
        preferred_element_type=jnp.float32,
    ) + lax.dot_general(
        partner_act, jnp.take(down_all, act_partner_from, axis=0), dims,
        preferred_element_type=jnp.float32,
    )
    down_w = down_all
    out_width = down_w.shape[2]
    produced = produced.astype(jnp.bfloat16).reshape(experts, 2 * slot_depth, out_width)
    returned = lax.all_to_all(produced, "expert", split_axis=0, concat_axis=0, tiled=True)
    id_match = (chosen[:, :, None] == expert_iota[None, None, :]).astype(jnp.int32)
    row_kept = jnp.sum(id_match * admitted[:, None, :], axis=2)
    row_main = jnp.sum(id_match * main_slot[:, None, :], axis=2)
    row_spill = jnp.sum(id_match * spill_slot[:, None, :], axis=2)
    row_other = jnp.sum(id_match * spill_row[None, None, :], axis=2)
    target = jnp.where(row_kept > 0, chosen, row_other)
    slot_pick = jnp.where(row_kept > 0, row_main, slot_depth + row_spill)
    row_index = target * (2 * slot_depth) + slot_pick
    picked = jnp.take(returned.reshape(-1, out_width), row_index.reshape(-1), axis=0).reshape(
        tok_rows, top_count, out_width
    )
    combined = jnp.sum(route_weight[0][:, :, None] * picked.astype(jnp.float32), axis=1).astype(
        jnp.bfloat16
    )
    forwarded = passed_along(combined, "section", 1)
    return forwarded[None]


def solution(mesh):
    in_specs = (
        P("section", "expert", "rep"),
        P("section", "expert", None),
        P("section", "expert", None),
        P("section", "expert"),
        P(),
        P("section", None),
        P("section", "expert", None, "rep"),
        P("section", "expert", None, "rep"),
        P("section", "expert", None, "rep"),
    )
    out_specs = P("section", "expert", "rep")
    return jax.shard_map(local, mesh=mesh, in_specs=in_specs, out_specs=out_specs, check_vma=False)
```

```python
import jax
import jax.numpy as jnp
from jax import lax
from jax.sharding import PartitionSpec as P


def passed_along(value, axis, steps):
    count = lax.axis_size(axis)
    pairs = [(source, (source + steps) % count) for source in range(count)]
    return lax.ppermute(value, axis, pairs)


def gathered(value, axis):
    count = lax.axis_size(axis)
    pieces = [value]
    for shift in range(1, count):
        pairs = [(source, (source + shift) % count) for source in range(count)]
        pieces.append(lax.ppermute(value, axis, pairs))
    return pieces


def chips_then_core(value, axis):
    count = lax.axis_size(axis)
    me = lax.axis_index(axis)
    pieces = [value]
    origins = [me]
    for shift in range(2, count, 2):
        pairs = [(source, (source + shift) % count) for source in range(count)]
        pieces.append(lax.ppermute(value, axis, pairs))
        origins.append((me - shift) % count)
    bundle = jnp.stack(pieces)
    swapped = lax.ppermute(bundle, axis, [(source, source ^ 1) for source in range(count)])
    origins = jnp.stack(origins)
    return bundle, swapped, origins, origins ^ 1


def relayed_chips_then_core(value, axis):
    count = lax.axis_size(axis)
    me = lax.axis_index(axis)
    up_pairs = [(source, (source + 2) % count) for source in range(count)]
    down_pairs = [(source, (source - 2) % count) for source in range(count)]
    from_below = lax.ppermute(value, axis, up_pairs)
    from_above = lax.ppermute(value, axis, down_pairs)
    half = value.shape[0] // 2
    far_low = lax.ppermute(from_below[:half], axis, up_pairs)
    far_high = lax.ppermute(from_above[half:], axis, down_pairs)
    far = jnp.concatenate([far_low, far_high], axis=0)
    bundle = jnp.stack([value, from_below, from_above, far])
    swapped = lax.ppermute(bundle, axis, [(source, source ^ 1) for source in range(count)])
    origins = jnp.stack([me, (me - 2) % count, (me + 2) % count, (me + 4) % count])
    return bundle, swapped, origins, origins ^ 1


def paired_gather(value, axis):
    count = lax.axis_size(axis)
    me = lax.axis_index(axis)
    partner = lax.ppermute(value, axis, [(source, source ^ 1) for source in range(count)])
    pair = jnp.stack([value, partner])
    pieces = [value, partner]
    origins = [me, me ^ 1]
    for shift in range(2, count, 2):
        pairs = [(source, (source + shift) % count) for source in range(count)]
        moved = lax.ppermute(pair, axis, pairs)
        origin = (me - shift) % count
        pieces.extend([moved[0], moved[1]])
        origins.extend([origin, origin ^ 1])
    return pieces, jnp.stack(origins)


def arrival_order(weight, axis):
    count = lax.axis_size(axis)
    me = lax.axis_index(axis)
    origin = (me - jnp.arange(count, dtype=jnp.int32)) % count
    return jnp.take(weight, origin, axis=0)


def admission(chosen, language, capacity, experts):
    lang_count = capacity.shape[0]
    hit_table = jnp.sum(
        (chosen[:, :, None] == jnp.arange(experts, dtype=jnp.int32)[None, None, :]).astype(
            jnp.int32
        ),
        axis=1,
    )
    lang_hot = (language[:, None] == jnp.arange(lang_count, dtype=jnp.int32)[None, :]).astype(
        jnp.int32
    )
    lang_hits = lang_hot[:, :, None] * hit_table[:, None, :]
    before = jnp.cumsum(lang_hits, axis=0) - lang_hits
    place_rank = jnp.sum(before * lang_hot[:, :, None], axis=1)
    allowance = jnp.sum(lang_hot[:, :, None] * capacity[None, :, :], axis=1)
    admitted = hit_table * (place_rank < allowance).astype(jnp.int32)
    return (hit_table, admitted)


def slot_sources(markers, slot_table, slot_depth):
    tok_rows = markers.shape[0]
    selected = markers[:, :, None] * (
        slot_table[:, :, None] == jnp.arange(slot_depth, dtype=jnp.int32)[None, None, :]
    ).astype(jnp.int32)
    positions = jnp.arange(tok_rows, dtype=jnp.int32)[:, None, None]
    source = jnp.sum(selected * positions, axis=0)
    filled = jnp.sum(selected, axis=0)
    return jnp.where(filled > 0, source, tok_rows)


def local(tokens, expert_ids, route_weight, language, capacity, spill_table, w_gate, w_up, w_down):
    experts = lax.axis_size("expert")
    reps = lax.axis_size("rep")
    chosen = expert_ids[0]
    spill_row = spill_table[0]
    tok_rows, top_count = chosen.shape
    slot_depth = min(tok_rows, max(2, 5 * tok_rows * top_count // (4 * experts)))
    expert_iota = jnp.arange(experts, dtype=jnp.int32)
    hit_table, admitted = admission(chosen, language[0], capacity, experts)
    spilled = hit_table - admitted
    main_slot = jnp.cumsum(admitted, axis=0) - admitted
    spill_slot = jnp.cumsum(spilled, axis=0) - spilled
    spill_move = (spill_row[:, None] == expert_iota[None, :]).astype(jnp.int32)
    spill_marks = jnp.sum(spilled[:, :, None] * spill_move[None, :, :], axis=1)
    spill_places = jnp.sum((spill_slot * spilled)[:, :, None] * spill_move[None, :, :], axis=1)
    rows_local = tokens[0]
    feat_width = rows_local.shape[1]
    main_source = slot_sources(admitted, main_slot, slot_depth)
    spill_source = slot_sources(spill_marks, spill_places, slot_depth)
    sources = jnp.concatenate([main_source, spill_source], axis=1)
    picks = (sources[:, :, None] == jnp.arange(tok_rows, dtype=jnp.int32)[None, None, :]).astype(
        rows_local.dtype
    )
    outgoing = jnp.einsum(
        "xjt,tf->xjf", picks, rows_local, preferred_element_type=jnp.float32
    ).astype(rows_local.dtype)
    arrived = lax.all_to_all(outgoing, "expert", split_axis=0, concat_axis=0, tiled=True)
    flattened = arrived.reshape(-1, feat_width)
    own_feats, partner_feats, own_from, partner_from = relayed_chips_then_core(flattened, "rep")
    hidden = w_gate.shape[3]
    gate_up = jnp.concatenate(
        [w_gate[0, 0].reshape(reps, feat_width, -1), w_up[0, 0].reshape(reps, feat_width, -1)],
        axis=2,
    )
    dims = (((0, 2), (0, 1)), ((), ()))
    both = lax.dot_general(
        own_feats, jnp.take(gate_up, own_from, axis=0), dims,
        preferred_element_type=jnp.float32,
    ) + lax.dot_general(
        partner_feats, jnp.take(gate_up, partner_from, axis=0), dims,
        preferred_element_type=jnp.float32,
    )
    gate_proj = both[:, :hidden]
    up_proj = both[:, hidden:]
    activated = (jax.nn.silu(gate_proj) * up_proj).astype(jnp.bfloat16)
    own_act, partner_act, act_own_from, act_partner_from = chips_then_core(activated, "rep")
    down_all = w_down[0, 0].reshape(reps, activated.shape[1], -1)
    produced = lax.dot_general(
        own_act, jnp.take(down_all, act_own_from, axis=0), dims,
        preferred_element_type=jnp.float32,
    ) + lax.dot_general(
        partner_act, jnp.take(down_all, act_partner_from, axis=0), dims,
        preferred_element_type=jnp.float32,
    )
    down_w = down_all
    out_width = down_w.shape[2]
    produced = produced.astype(jnp.bfloat16).reshape(experts, 2 * slot_depth, out_width)
    returned = lax.all_to_all(produced, "expert", split_axis=0, concat_axis=0, tiled=True)
    id_match = (chosen[:, :, None] == expert_iota[None, None, :]).astype(jnp.int32)
    row_kept = jnp.sum(id_match * admitted[:, None, :], axis=2)
    row_main = jnp.sum(id_match * main_slot[:, None, :], axis=2)
    row_spill = jnp.sum(id_match * spill_slot[:, None, :], axis=2)
    row_other = jnp.sum(id_match * spill_row[None, None, :], axis=2)
    target = jnp.where(row_kept > 0, chosen, row_other)
    slot_pick = jnp.where(row_kept > 0, row_main, slot_depth + row_spill)
    row_index = target * (2 * slot_depth) + slot_pick
    picked = jnp.take(returned.reshape(-1, out_width), row_index.reshape(-1), axis=0).reshape(
        tok_rows, top_count, out_width
    )
    combined = jnp.sum(route_weight[0][:, :, None] * picked.astype(jnp.float32), axis=1).astype(
        jnp.bfloat16
    )
    forwarded = passed_along(combined, "section", 1)
    return forwarded[None]


def solution(mesh):
    in_specs = (
        P("section", "expert", "rep"),
        P("section", "expert", None),
        P("section", "expert", None),
        P("section", "expert"),
        P(),
        P("section", None),
        P("section", "expert", None, "rep"),
        P("section", "expert", None, "rep"),
        P("section", "expert", None, "rep"),
    )
    out_specs = P("section", "expert", "rep")
    return jax.shard_map(local, mesh=mesh, in_specs=in_specs, out_specs=out_specs, check_vma=False)
```

```python
import jax
import jax.numpy as jnp
from jax import lax
from jax.sharding import PartitionSpec as P


def passed_along(value, axis, steps):
    count = lax.axis_size(axis)
    pairs = [(source, (source + steps) % count) for source in range(count)]
    return lax.ppermute(value, axis, pairs)


def gathered(value, axis):
    count = lax.axis_size(axis)
    pieces = [value]
    for shift in range(1, count):
        pairs = [(source, (source + shift) % count) for source in range(count)]
        pieces.append(lax.ppermute(value, axis, pairs))
    return pieces


def chips_then_core(value, axis):
    count = lax.axis_size(axis)
    me = lax.axis_index(axis)
    pieces = [value]
    origins = [me]
    for shift in range(2, count, 2):
        pairs = [(source, (source + shift) % count) for source in range(count)]
        pieces.append(lax.ppermute(value, axis, pairs))
        origins.append((me - shift) % count)
    bundle = jnp.stack(pieces)
    swapped = lax.ppermute(bundle, axis, [(source, source ^ 1) for source in range(count)])
    origins = jnp.stack(origins)
    return bundle, swapped, origins, origins ^ 1


def relayed_chips_then_core(value, axis):
    count = lax.axis_size(axis)
    me = lax.axis_index(axis)
    up_pairs = [(source, (source + 2) % count) for source in range(count)]
    down_pairs = [(source, (source - 2) % count) for source in range(count)]
    from_below = lax.ppermute(value, axis, up_pairs)
    from_above = lax.ppermute(value, axis, down_pairs)
    half = value.shape[0] // 2
    far_low = lax.ppermute(from_below[:half], axis, up_pairs)
    far_high = lax.ppermute(from_above[half:], axis, down_pairs)
    far = jnp.concatenate([far_low, far_high], axis=0)
    bundle = jnp.stack([value, from_below, from_above, far])
    swapped = lax.ppermute(bundle, axis, [(source, source ^ 1) for source in range(count)])
    origins = jnp.stack([me, (me - 2) % count, (me + 2) % count, (me + 4) % count])
    return bundle, swapped, origins, origins ^ 1


def relayed_in_two_swaps(value, axis):
    count = lax.axis_size(axis)
    me = lax.axis_index(axis)
    up_pairs = [(source, (source + 2) % count) for source in range(count)]
    down_pairs = [(source, (source - 2) % count) for source in range(count)]
    swap_pairs = [(source, source ^ 1) for source in range(count)]
    from_below = lax.ppermute(value, axis, up_pairs)
    from_above = lax.ppermute(value, axis, down_pairs)
    half = value.shape[0] // 2
    far_low = lax.ppermute(from_below[:half], axis, up_pairs)
    far_high = lax.ppermute(from_above[half:], axis, down_pairs)
    near = jnp.stack([value, from_below, from_above])
    near_swapped = lax.ppermute(near, axis, swap_pairs)
    far = jnp.concatenate([far_low, far_high], axis=0)[None]
    far_swapped = lax.ppermute(far, axis, swap_pairs)
    near_from = jnp.stack([me, (me - 2) % count, (me + 2) % count])
    far_from = ((me + 4) % count)[None]
    return [
        (near, near_from),
        (near_swapped, near_from ^ 1),
        (far, far_from),
        (far_swapped, far_from ^ 1),
    ]


def paired_gather(value, axis):
    count = lax.axis_size(axis)
    me = lax.axis_index(axis)
    partner = lax.ppermute(value, axis, [(source, source ^ 1) for source in range(count)])
    pair = jnp.stack([value, partner])
    pieces = [value, partner]
    origins = [me, me ^ 1]
    for shift in range(2, count, 2):
        pairs = [(source, (source + shift) % count) for source in range(count)]
        moved = lax.ppermute(pair, axis, pairs)
        origin = (me - shift) % count
        pieces.extend([moved[0], moved[1]])
        origins.extend([origin, origin ^ 1])
    return pieces, jnp.stack(origins)


def arrival_order(weight, axis):
    count = lax.axis_size(axis)
    me = lax.axis_index(axis)
    origin = (me - jnp.arange(count, dtype=jnp.int32)) % count
    return jnp.take(weight, origin, axis=0)


def admission(chosen, language, capacity, experts):
    lang_count = capacity.shape[0]
    hit_table = jnp.sum(
        (chosen[:, :, None] == jnp.arange(experts, dtype=jnp.int32)[None, None, :]).astype(
            jnp.int32
        ),
        axis=1,
    )
    lang_hot = (language[:, None] == jnp.arange(lang_count, dtype=jnp.int32)[None, :]).astype(
        jnp.int32
    )
    lang_hits = lang_hot[:, :, None] * hit_table[:, None, :]
    before = jnp.cumsum(lang_hits, axis=0) - lang_hits
    place_rank = jnp.sum(before * lang_hot[:, :, None], axis=1)
    allowance = jnp.sum(lang_hot[:, :, None] * capacity[None, :, :], axis=1)
    admitted = hit_table * (place_rank < allowance).astype(jnp.int32)
    return (hit_table, admitted)


def slot_sources(markers, slot_table, slot_depth):
    tok_rows = markers.shape[0]
    selected = markers[:, :, None] * (
        slot_table[:, :, None] == jnp.arange(slot_depth, dtype=jnp.int32)[None, None, :]
    ).astype(jnp.int32)
    positions = jnp.arange(tok_rows, dtype=jnp.int32)[:, None, None]
    source = jnp.sum(selected * positions, axis=0)
    filled = jnp.sum(selected, axis=0)
    return jnp.where(filled > 0, source, tok_rows)


def local(tokens, expert_ids, route_weight, language, capacity, spill_table, w_gate, w_up, w_down):
    experts = lax.axis_size("expert")
    reps = lax.axis_size("rep")
    chosen = expert_ids[0]
    spill_row = spill_table[0]
    tok_rows, top_count = chosen.shape
    slot_depth = min(tok_rows, max(2, 5 * tok_rows * top_count // (4 * experts)))
    expert_iota = jnp.arange(experts, dtype=jnp.int32)
    hit_table, admitted = admission(chosen, language[0], capacity, experts)
    spilled = hit_table - admitted
    main_slot = jnp.cumsum(admitted, axis=0) - admitted
    spill_slot = jnp.cumsum(spilled, axis=0) - spilled
    spill_move = (spill_row[:, None] == expert_iota[None, :]).astype(jnp.int32)
    spill_marks = jnp.sum(spilled[:, :, None] * spill_move[None, :, :], axis=1)
    spill_places = jnp.sum((spill_slot * spilled)[:, :, None] * spill_move[None, :, :], axis=1)
    rows_local = tokens[0]
    feat_width = rows_local.shape[1]
    main_source = slot_sources(admitted, main_slot, slot_depth)
    spill_source = slot_sources(spill_marks, spill_places, slot_depth)
    sources = jnp.concatenate([main_source, spill_source], axis=1)
    picks = (sources[:, :, None] == jnp.arange(tok_rows, dtype=jnp.int32)[None, None, :]).astype(
        rows_local.dtype
    )
    outgoing = jnp.einsum(
        "xjt,tf->xjf", picks, rows_local, preferred_element_type=jnp.float32
    ).astype(rows_local.dtype)
    arrived = lax.all_to_all(outgoing, "expert", split_axis=0, concat_axis=0, tiled=True)
    flattened = arrived.reshape(-1, feat_width)
    row_pieces = relayed_in_two_swaps(flattened, "rep")
    hidden = w_gate.shape[3]
    gate_up = jnp.concatenate(
        [w_gate[0, 0].reshape(reps, feat_width, -1), w_up[0, 0].reshape(reps, feat_width, -1)],
        axis=2,
    )
    dims = (((0, 2), (0, 1)), ((), ()))
    both = None
    for piece, origin in row_pieces:
        term = lax.dot_general(
            piece, jnp.take(gate_up, origin, axis=0), dims, preferred_element_type=jnp.float32
        )
        both = term if both is None else both + term
    gate_proj = both[:, :hidden]
    up_proj = both[:, hidden:]
    activated = (jax.nn.silu(gate_proj) * up_proj).astype(jnp.bfloat16)
    own_act, partner_act, act_own_from, act_partner_from = chips_then_core(activated, "rep")
    down_all = w_down[0, 0].reshape(reps, activated.shape[1], -1)
    produced = lax.dot_general(
        own_act, jnp.take(down_all, act_own_from, axis=0), dims,
        preferred_element_type=jnp.float32,
    ) + lax.dot_general(
        partner_act, jnp.take(down_all, act_partner_from, axis=0), dims,
        preferred_element_type=jnp.float32,
    )
    down_w = down_all
    out_width = down_w.shape[2]
    produced = produced.astype(jnp.bfloat16).reshape(experts, 2 * slot_depth, out_width)
    returned = lax.all_to_all(produced, "expert", split_axis=0, concat_axis=0, tiled=True)
    id_match = (chosen[:, :, None] == expert_iota[None, None, :]).astype(jnp.int32)
    row_kept = jnp.sum(id_match * admitted[:, None, :], axis=2)
    row_main = jnp.sum(id_match * main_slot[:, None, :], axis=2)
    row_spill = jnp.sum(id_match * spill_slot[:, None, :], axis=2)
    row_other = jnp.sum(id_match * spill_row[None, None, :], axis=2)
    target = jnp.where(row_kept > 0, chosen, row_other)
    slot_pick = jnp.where(row_kept > 0, row_main, slot_depth + row_spill)
    row_index = target * (2 * slot_depth) + slot_pick
    picked = jnp.take(returned.reshape(-1, out_width), row_index.reshape(-1), axis=0).reshape(
        tok_rows, top_count, out_width
    )
    combined = jnp.sum(route_weight[0][:, :, None] * picked.astype(jnp.float32), axis=1).astype(
        jnp.bfloat16
    )
    forwarded = passed_along(combined, "section", 1)
    return forwarded[None]


def solution(mesh):
    in_specs = (
        P("section", "expert", "rep"),
        P("section", "expert", None),
        P("section", "expert", None),
        P("section", "expert"),
        P(),
        P("section", None),
        P("section", "expert", None, "rep"),
        P("section", "expert", None, "rep"),
        P("section", "expert", None, "rep"),
    )
    out_specs = P("section", "expert", "rep")
    return jax.shard_map(local, mesh=mesh, in_specs=in_specs, out_specs=out_specs, check_vma=False)
```

```python
import jax
import jax.numpy as jnp
from jax import lax
from jax.sharding import PartitionSpec as P


def passed_along(value, axis, steps):
    count = lax.axis_size(axis)
    pairs = [(source, (source + steps) % count) for source in range(count)]
    return lax.ppermute(value, axis, pairs)


def gathered(value, axis):
    count = lax.axis_size(axis)
    pieces = [value]
    for shift in range(1, count):
        pairs = [(source, (source + shift) % count) for source in range(count)]
        pieces.append(lax.ppermute(value, axis, pairs))
    return pieces


def chips_then_core(value, axis):
    count = lax.axis_size(axis)
    me = lax.axis_index(axis)
    pieces = [value]
    origins = [me]
    for shift in range(2, count, 2):
        pairs = [(source, (source + shift) % count) for source in range(count)]
        pieces.append(lax.ppermute(value, axis, pairs))
        origins.append((me - shift) % count)
    bundle = jnp.stack(pieces)
    swapped = lax.ppermute(bundle, axis, [(source, source ^ 1) for source in range(count)])
    origins = jnp.stack(origins)
    return bundle, swapped, origins, origins ^ 1


def relayed_chips_then_core(value, axis, riders):
    count = lax.axis_size(axis)
    me = lax.axis_index(axis)
    up_pairs = [(source, (source + 2) % count) for source in range(count)]
    down_pairs = [(source, (source - 2) % count) for source in range(count)]
    from_below = lax.ppermute(value, axis, up_pairs)
    from_above = lax.ppermute(value, axis, down_pairs)
    from_below, from_above, riders = lax.optimization_barrier((from_below, from_above, riders))
    half = value.shape[0] // 2
    far_low = lax.ppermute(from_below[:half], axis, up_pairs)
    far_high = lax.ppermute(from_above[half:], axis, down_pairs)
    far = jnp.concatenate([far_low, far_high], axis=0)
    bundle = jnp.stack([value, from_below, from_above, far])
    swapped = lax.ppermute(bundle, axis, [(source, source ^ 1) for source in range(count)])
    return bundle, swapped, riders


def paired_gather(value, axis):
    count = lax.axis_size(axis)
    me = lax.axis_index(axis)
    partner = lax.ppermute(value, axis, [(source, source ^ 1) for source in range(count)])
    pair = jnp.stack([value, partner])
    pieces = [value, partner]
    origins = [me, me ^ 1]
    for shift in range(2, count, 2):
        pairs = [(source, (source + shift) % count) for source in range(count)]
        moved = lax.ppermute(pair, axis, pairs)
        origin = (me - shift) % count
        pieces.extend([moved[0], moved[1]])
        origins.extend([origin, origin ^ 1])
    return pieces, jnp.stack(origins)


def arrival_order(weight, axis):
    count = lax.axis_size(axis)
    me = lax.axis_index(axis)
    origin = (me - jnp.arange(count, dtype=jnp.int32)) % count
    return jnp.take(weight, origin, axis=0)


def admission(chosen, language, capacity, experts):
    lang_count = capacity.shape[0]
    hit_table = jnp.sum(
        (chosen[:, :, None] == jnp.arange(experts, dtype=jnp.int32)[None, None, :]).astype(
            jnp.int32
        ),
        axis=1,
    )
    lang_hot = (language[:, None] == jnp.arange(lang_count, dtype=jnp.int32)[None, :]).astype(
        jnp.int32
    )
    lang_hits = lang_hot[:, :, None] * hit_table[:, None, :]
    before = jnp.cumsum(lang_hits, axis=0) - lang_hits
    place_rank = jnp.sum(before * lang_hot[:, :, None], axis=1)
    allowance = jnp.sum(lang_hot[:, :, None] * capacity[None, :, :], axis=1)
    admitted = hit_table * (place_rank < allowance).astype(jnp.int32)
    return (hit_table, admitted)


def slot_sources(markers, slot_table, slot_depth):
    tok_rows = markers.shape[0]
    selected = markers[:, :, None] * (
        slot_table[:, :, None] == jnp.arange(slot_depth, dtype=jnp.int32)[None, None, :]
    ).astype(jnp.int32)
    positions = jnp.arange(tok_rows, dtype=jnp.int32)[:, None, None]
    source = jnp.sum(selected * positions, axis=0)
    filled = jnp.sum(selected, axis=0)
    return jnp.where(filled > 0, source, tok_rows)


def local(tokens, expert_ids, route_weight, language, capacity, spill_table, w_gate, w_up, w_down):
    experts = lax.axis_size("expert")
    reps = lax.axis_size("rep")
    chosen = expert_ids[0]
    spill_row = spill_table[0]
    tok_rows, top_count = chosen.shape
    slot_depth = min(tok_rows, max(2, 5 * tok_rows * top_count // (4 * experts)))
    expert_iota = jnp.arange(experts, dtype=jnp.int32)
    hit_table, admitted = admission(chosen, language[0], capacity, experts)
    spilled = hit_table - admitted
    main_slot = jnp.cumsum(admitted, axis=0) - admitted
    spill_slot = jnp.cumsum(spilled, axis=0) - spilled
    spill_move = (spill_row[:, None] == expert_iota[None, :]).astype(jnp.int32)
    spill_marks = jnp.sum(spilled[:, :, None] * spill_move[None, :, :], axis=1)
    spill_places = jnp.sum((spill_slot * spilled)[:, :, None] * spill_move[None, :, :], axis=1)
    rows_local = tokens[0]
    feat_width = rows_local.shape[1]
    main_source = slot_sources(admitted, main_slot, slot_depth)
    spill_source = slot_sources(spill_marks, spill_places, slot_depth)
    sources = jnp.concatenate([main_source, spill_source], axis=1)
    picks = (sources[:, :, None] == jnp.arange(tok_rows, dtype=jnp.int32)[None, None, :]).astype(
        rows_local.dtype
    )
    outgoing = jnp.einsum(
        "xjt,tf->xjf", picks, rows_local, preferred_element_type=jnp.float32
    ).astype(rows_local.dtype)
    arrived = lax.all_to_all(outgoing, "expert", split_axis=0, concat_axis=0, tiled=True)
    flattened = arrived.reshape(-1, feat_width)
    me_rep = lax.axis_index("rep")
    rows_from = jnp.stack([me_rep, (me_rep - 2) % reps, (me_rep + 2) % reps, (me_rep + 4) % reps])
    act_from = (me_rep - 2 * jnp.arange(reps // 2, dtype=jnp.int32)) % reps
    hidden = w_gate.shape[3]
    gate_up = jnp.concatenate(
        [w_gate[0, 0].reshape(reps, feat_width, -1), w_up[0, 0].reshape(reps, feat_width, -1)],
        axis=2,
    )
    down_all = w_down[0, 0].reshape(reps, hidden, -1)
    riders = (
        jnp.take(gate_up, rows_from, axis=0),
        jnp.take(gate_up, rows_from ^ 1, axis=0),
        jnp.take(down_all, act_from, axis=0),
        jnp.take(down_all, act_from ^ 1, axis=0),
    )
    own_feats, partner_feats, riders = relayed_chips_then_core(flattened, "rep", riders)
    gu_own, gu_partner, down_own, down_partner = riders
    dims = (((0, 2), (0, 1)), ((), ()))
    both = lax.dot_general(
        own_feats, gu_own, dims, preferred_element_type=jnp.float32
    ) + lax.dot_general(partner_feats, gu_partner, dims, preferred_element_type=jnp.float32)
    gate_proj = both[:, :hidden]
    up_proj = both[:, hidden:]
    activated = (jax.nn.silu(gate_proj) * up_proj).astype(jnp.bfloat16)
    own_act, partner_act, _, _ = chips_then_core(activated, "rep")
    produced = lax.dot_general(
        own_act, down_own, dims, preferred_element_type=jnp.float32
    ) + lax.dot_general(partner_act, down_partner, dims, preferred_element_type=jnp.float32)
    down_w = down_all
    out_width = down_w.shape[2]
    produced = produced.astype(jnp.bfloat16).reshape(experts, 2 * slot_depth, out_width)
    returned = lax.all_to_all(produced, "expert", split_axis=0, concat_axis=0, tiled=True)
    id_match = (chosen[:, :, None] == expert_iota[None, None, :]).astype(jnp.int32)
    row_kept = jnp.sum(id_match * admitted[:, None, :], axis=2)
    row_main = jnp.sum(id_match * main_slot[:, None, :], axis=2)
    row_spill = jnp.sum(id_match * spill_slot[:, None, :], axis=2)
    row_other = jnp.sum(id_match * spill_row[None, None, :], axis=2)
    target = jnp.where(row_kept > 0, chosen, row_other)
    slot_pick = jnp.where(row_kept > 0, row_main, slot_depth + row_spill)
    row_index = target * (2 * slot_depth) + slot_pick
    picked = jnp.take(returned.reshape(-1, out_width), row_index.reshape(-1), axis=0).reshape(
        tok_rows, top_count, out_width
    )
    combined = jnp.sum(route_weight[0][:, :, None] * picked.astype(jnp.float32), axis=1).astype(
        jnp.bfloat16
    )
    forwarded = passed_along(combined, "section", 1)
    return forwarded[None]


def solution(mesh):
    in_specs = (
        P("section", "expert", "rep"),
        P("section", "expert", None),
        P("section", "expert", None),
        P("section", "expert"),
        P(),
        P("section", None),
        P("section", "expert", None, "rep"),
        P("section", "expert", None, "rep"),
        P("section", "expert", None, "rep"),
    )
    out_specs = P("section", "expert", "rep")
    return jax.shard_map(local, mesh=mesh, in_specs=in_specs, out_specs=out_specs, check_vma=False)
```

```python
import jax
import jax.numpy as jnp
from jax import lax
from jax.sharding import PartitionSpec as P


def passed_along(value, axis, steps):
    count = lax.axis_size(axis)
    pairs = [(source, (source + steps) % count) for source in range(count)]
    return lax.ppermute(value, axis, pairs)


def gathered(value, axis):
    count = lax.axis_size(axis)
    pieces = [value]
    for shift in range(1, count):
        pairs = [(source, (source + shift) % count) for source in range(count)]
        pieces.append(lax.ppermute(value, axis, pairs))
    return pieces


def chips_then_core(value, axis):
    count = lax.axis_size(axis)
    me = lax.axis_index(axis)
    pieces = [value]
    origins = [me]
    for shift in range(2, count, 2):
        pairs = [(source, (source + shift) % count) for source in range(count)]
        pieces.append(lax.ppermute(value, axis, pairs))
        origins.append((me - shift) % count)
    bundle = jnp.stack(pieces)
    swapped = lax.ppermute(bundle, axis, [(source, source ^ 1) for source in range(count)])
    origins = jnp.stack(origins)
    return bundle, swapped, origins, origins ^ 1


def relayed_chips_then_core(value, axis):
    count = lax.axis_size(axis)
    me = lax.axis_index(axis)
    up_pairs = [(source, (source + 2) % count) for source in range(count)]
    down_pairs = [(source, (source - 2) % count) for source in range(count)]
    from_below = lax.ppermute(value, axis, up_pairs)
    from_above = lax.ppermute(value, axis, down_pairs)
    half = value.shape[0] // 2
    far_low = lax.ppermute(from_below[:half], axis, up_pairs)
    far_high = lax.ppermute(from_above[half:], axis, down_pairs)
    far = jnp.concatenate([far_low, far_high], axis=0)
    bundle = jnp.stack([value, from_below, from_above, far])
    swapped = lax.ppermute(bundle, axis, [(source, source ^ 1) for source in range(count)])
    origins = jnp.stack([me, (me - 2) % count, (me + 2) % count, (me + 4) % count])
    return bundle, swapped, origins, origins ^ 1


def paired_gather(value, axis):
    count = lax.axis_size(axis)
    me = lax.axis_index(axis)
    partner = lax.ppermute(value, axis, [(source, source ^ 1) for source in range(count)])
    pair = jnp.stack([value, partner])
    pieces = [value, partner]
    origins = [me, me ^ 1]
    for shift in range(2, count, 2):
        pairs = [(source, (source + shift) % count) for source in range(count)]
        moved = lax.ppermute(pair, axis, pairs)
        origin = (me - shift) % count
        pieces.extend([moved[0], moved[1]])
        origins.extend([origin, origin ^ 1])
    return pieces, jnp.stack(origins)


def arrival_order(weight, axis):
    count = lax.axis_size(axis)
    me = lax.axis_index(axis)
    origin = (me - jnp.arange(count, dtype=jnp.int32)) % count
    return jnp.take(weight, origin, axis=0)


def admission(chosen, language, capacity, experts):
    lang_count = capacity.shape[0]
    hit_table = jnp.sum(
        (chosen[:, :, None] == jnp.arange(experts, dtype=jnp.int32)[None, None, :]).astype(
            jnp.int32
        ),
        axis=1,
    )
    lang_hot = (language[:, None] == jnp.arange(lang_count, dtype=jnp.int32)[None, :]).astype(
        jnp.int32
    )
    lang_hits = lang_hot[:, :, None] * hit_table[:, None, :]
    before = jnp.cumsum(lang_hits, axis=0) - lang_hits
    place_rank = jnp.sum(before * lang_hot[:, :, None], axis=1)
    allowance = jnp.sum(lang_hot[:, :, None] * capacity[None, :, :], axis=1)
    admitted = hit_table * (place_rank < allowance).astype(jnp.int32)
    return (hit_table, admitted)


def slot_sources(markers, slot_table, slot_depth):
    tok_rows = markers.shape[0]
    selected = markers[:, :, None] * (
        slot_table[:, :, None] == jnp.arange(slot_depth, dtype=jnp.int32)[None, None, :]
    ).astype(jnp.int32)
    positions = jnp.arange(tok_rows, dtype=jnp.int32)[:, None, None]
    source = jnp.sum(selected * positions, axis=0)
    filled = jnp.sum(selected, axis=0)
    return jnp.where(filled > 0, source, tok_rows)


def local(tokens, expert_ids, route_weight, language, capacity, spill_table, w_gate, w_up, w_down):
    experts = lax.axis_size("expert")
    reps = lax.axis_size("rep")
    chosen = expert_ids[0]
    spill_row = spill_table[0]
    tok_rows, top_count = chosen.shape
    slot_depth = min(tok_rows, max(2, 5 * tok_rows * top_count // (4 * experts)))
    expert_iota = jnp.arange(experts, dtype=jnp.int32)
    hit_table, admitted = admission(chosen, language[0], capacity, experts)
    spilled = hit_table - admitted
    main_slot = jnp.cumsum(admitted, axis=0) - admitted
    spill_slot = jnp.cumsum(spilled, axis=0) - spilled
    spill_move = (spill_row[:, None] == expert_iota[None, :]).astype(jnp.int32)
    spill_marks = jnp.sum(spilled[:, :, None] * spill_move[None, :, :], axis=1)
    spill_places = jnp.sum((spill_slot * spilled)[:, :, None] * spill_move[None, :, :], axis=1)
    rows_local = tokens[0]
    feat_width = rows_local.shape[1]
    main_source = slot_sources(admitted, main_slot, slot_depth)
    spill_source = slot_sources(spill_marks, spill_places, slot_depth)
    sources = jnp.concatenate([main_source, spill_source], axis=1)
    picks = (sources[:, :, None] == jnp.arange(tok_rows, dtype=jnp.int32)[None, None, :]).astype(
        rows_local.dtype
    )
    outgoing = jnp.einsum(
        "xjt,tf->xjf", picks, rows_local, preferred_element_type=jnp.float32
    ).astype(rows_local.dtype)
    arrived = lax.all_to_all(outgoing, "expert", split_axis=0, concat_axis=0, tiled=True)
    flattened = arrived.reshape(-1, feat_width)
    own_feats, partner_feats, own_from, partner_from = relayed_chips_then_core(flattened, "rep")
    hidden = w_gate.shape[3]
    gate_up = jnp.concatenate(
        [w_gate[0, 0].reshape(reps, feat_width, -1), w_up[0, 0].reshape(reps, feat_width, -1)],
        axis=2,
    )
    dims = (((0, 2), (0, 1)), ((), ()))
    both = lax.dot_general(
        own_feats, jnp.take(gate_up, own_from, axis=0), dims,
        preferred_element_type=jnp.float32,
    ) + lax.dot_general(
        partner_feats, jnp.take(gate_up, partner_from, axis=0), dims,
        preferred_element_type=jnp.float32,
    )
    gate_proj = both[:, :hidden]
    up_proj = both[:, hidden:]
    activated = (jax.nn.silu(gate_proj) * up_proj).astype(jnp.bfloat16)
    own_act, partner_act, act_own_from, act_partner_from = relayed_chips_then_core(
        activated, "rep"
    )
    down_all = w_down[0, 0].reshape(reps, activated.shape[1], -1)
    produced = lax.dot_general(
        own_act, jnp.take(down_all, act_own_from, axis=0), dims,
        preferred_element_type=jnp.float32,
    ) + lax.dot_general(
        partner_act, jnp.take(down_all, act_partner_from, axis=0), dims,
        preferred_element_type=jnp.float32,
    )
    down_w = down_all
    out_width = down_w.shape[2]
    produced = produced.astype(jnp.bfloat16).reshape(experts, 2 * slot_depth, out_width)
    returned = lax.all_to_all(produced, "expert", split_axis=0, concat_axis=0, tiled=True)
    id_match = (chosen[:, :, None] == expert_iota[None, None, :]).astype(jnp.int32)
    row_kept = jnp.sum(id_match * admitted[:, None, :], axis=2)
    row_main = jnp.sum(id_match * main_slot[:, None, :], axis=2)
    row_spill = jnp.sum(id_match * spill_slot[:, None, :], axis=2)
    row_other = jnp.sum(id_match * spill_row[None, None, :], axis=2)
    target = jnp.where(row_kept > 0, chosen, row_other)
    slot_pick = jnp.where(row_kept > 0, row_main, slot_depth + row_spill)
    row_index = target * (2 * slot_depth) + slot_pick
    picked = jnp.take(returned.reshape(-1, out_width), row_index.reshape(-1), axis=0).reshape(
        tok_rows, top_count, out_width
    )
    combined = jnp.sum(route_weight[0][:, :, None] * picked.astype(jnp.float32), axis=1).astype(
        jnp.bfloat16
    )
    forwarded = passed_along(combined, "section", 1)
    return forwarded[None]


def solution(mesh):
    in_specs = (
        P("section", "expert", "rep"),
        P("section", "expert", None),
        P("section", "expert", None),
        P("section", "expert"),
        P(),
        P("section", None),
        P("section", "expert", None, "rep"),
        P("section", "expert", None, "rep"),
        P("section", "expert", None, "rep"),
    )
    out_specs = P("section", "expert", "rep")
    return jax.shard_map(local, mesh=mesh, in_specs=in_specs, out_specs=out_specs, check_vma=False)
```

```python
import jax
import jax.numpy as jnp
from jax import lax
from jax.sharding import PartitionSpec as P


def passed_along(value, axis, steps):
    count = lax.axis_size(axis)
    pairs = [(source, (source + steps) % count) for source in range(count)]
    return lax.ppermute(value, axis, pairs)


def gathered(value, axis):
    count = lax.axis_size(axis)
    pieces = [value]
    for shift in range(1, count):
        pairs = [(source, (source + shift) % count) for source in range(count)]
        pieces.append(lax.ppermute(value, axis, pairs))
    return pieces


def chips_then_core(value, axis):
    count = lax.axis_size(axis)
    me = lax.axis_index(axis)
    pieces = [value]
    origins = [me]
    for shift in range(2, count, 2):
        pairs = [(source, (source + shift) % count) for source in range(count)]
        pieces.append(lax.ppermute(value, axis, pairs))
        origins.append((me - shift) % count)
    bundle = jnp.stack(pieces)
    swapped = lax.ppermute(bundle, axis, [(source, source ^ 1) for source in range(count)])
    origins = jnp.stack(origins)
    return bundle, swapped, origins, origins ^ 1


def relayed_chips_then_core(value, axis):
    count = lax.axis_size(axis)
    me = lax.axis_index(axis)
    up_pairs = [(source, (source + 2) % count) for source in range(count)]
    down_pairs = [(source, (source - 2) % count) for source in range(count)]
    from_below = lax.ppermute(value, axis, up_pairs)
    from_above = lax.ppermute(value, axis, down_pairs)
    half = value.shape[0] // 2
    far_low = lax.ppermute(from_below[:half], axis, up_pairs)
    far_high = lax.ppermute(from_above[half:], axis, down_pairs)
    far = jnp.concatenate([far_low, far_high], axis=0)
    bundle = jnp.stack([value, from_below, from_above, far])
    swapped = lax.ppermute(bundle, axis, [(source, source ^ 1) for source in range(count)])
    origins = jnp.stack([me, (me - 2) % count, (me + 2) % count, (me + 4) % count])
    return bundle, swapped, origins, origins ^ 1


def paired_gather(value, axis):
    count = lax.axis_size(axis)
    me = lax.axis_index(axis)
    partner = lax.ppermute(value, axis, [(source, source ^ 1) for source in range(count)])
    pair = jnp.stack([value, partner])
    pieces = [value, partner]
    origins = [me, me ^ 1]
    for shift in range(2, count, 2):
        pairs = [(source, (source + shift) % count) for source in range(count)]
        moved = lax.ppermute(pair, axis, pairs)
        origin = (me - shift) % count
        pieces.extend([moved[0], moved[1]])
        origins.extend([origin, origin ^ 1])
    return pieces, jnp.stack(origins)


def arrival_order(weight, axis):
    count = lax.axis_size(axis)
    me = lax.axis_index(axis)
    origin = (me - jnp.arange(count, dtype=jnp.int32)) % count
    return jnp.take(weight, origin, axis=0)


def admission(chosen, language, capacity, experts):
    lang_count = capacity.shape[0]
    hit_table = jnp.sum(
        (chosen[:, :, None] == jnp.arange(experts, dtype=jnp.int32)[None, None, :]).astype(
            jnp.int32
        ),
        axis=1,
    )
    lang_hot = (language[:, None] == jnp.arange(lang_count, dtype=jnp.int32)[None, :]).astype(
        jnp.int32
    )
    lang_hits = lang_hot[:, :, None] * hit_table[:, None, :]
    before = jnp.cumsum(lang_hits, axis=0) - lang_hits
    place_rank = jnp.sum(before * lang_hot[:, :, None], axis=1)
    allowance = jnp.sum(lang_hot[:, :, None] * capacity[None, :, :], axis=1)
    admitted = hit_table * (place_rank < allowance).astype(jnp.int32)
    return (hit_table, admitted)


def slot_sources(markers, slot_table, slot_depth):
    tok_rows = markers.shape[0]
    selected = markers[:, :, None] * (
        slot_table[:, :, None] == jnp.arange(slot_depth, dtype=jnp.int32)[None, None, :]
    ).astype(jnp.int32)
    positions = jnp.arange(tok_rows, dtype=jnp.int32)[:, None, None]
    source = jnp.sum(selected * positions, axis=0)
    filled = jnp.sum(selected, axis=0)
    return jnp.where(filled > 0, source, tok_rows)


def local(tokens, expert_ids, route_weight, language, capacity, spill_table, w_gate, w_up, w_down):
    experts = lax.axis_size("expert")
    reps = lax.axis_size("rep")
    chosen = expert_ids[0]
    spill_row = spill_table[0]
    tok_rows, top_count = chosen.shape
    slot_depth = min(tok_rows, max(2, 5 * tok_rows * top_count // (4 * experts)))
    expert_iota = jnp.arange(experts, dtype=jnp.int32)
    hit_table, admitted = admission(chosen, language[0], capacity, experts)
    spilled = hit_table - admitted
    main_slot = jnp.cumsum(admitted, axis=0) - admitted
    spill_slot = jnp.cumsum(spilled, axis=0) - spilled
    spill_move = (spill_row[:, None] == expert_iota[None, :]).astype(jnp.int32)
    spill_marks = jnp.sum(spilled[:, :, None] * spill_move[None, :, :], axis=1)
    spill_places = jnp.sum((spill_slot * spilled)[:, :, None] * spill_move[None, :, :], axis=1)
    rows_local = tokens[0]
    feat_width = rows_local.shape[1]
    slot_iota = jnp.arange(slot_depth, dtype=jnp.int32)
    main_picks = admitted.T[:, None, :] * (main_slot.T[:, None, :] == slot_iota[None, :, None])
    spill_picks = spill_marks.T[:, None, :] * (
        spill_places.T[:, None, :] == slot_iota[None, :, None]
    )
    picks = jnp.concatenate([main_picks, spill_picks], axis=1).astype(rows_local.dtype)
    outgoing = jnp.einsum(
        "xjt,tf->xjf", picks, rows_local, preferred_element_type=jnp.float32
    ).astype(rows_local.dtype)
    arrived = lax.all_to_all(outgoing, "expert", split_axis=0, concat_axis=0, tiled=True)
    flattened = arrived.reshape(-1, feat_width)
    own_feats, partner_feats, own_from, partner_from = relayed_chips_then_core(flattened, "rep")
    hidden = w_gate.shape[3]
    gate_up = jnp.concatenate(
        [w_gate[0, 0].reshape(reps, feat_width, -1), w_up[0, 0].reshape(reps, feat_width, -1)],
        axis=2,
    )
    dims = (((0, 2), (0, 1)), ((), ()))
    both = lax.dot_general(
        own_feats, jnp.take(gate_up, own_from, axis=0), dims,
        preferred_element_type=jnp.float32,
    ) + lax.dot_general(
        partner_feats, jnp.take(gate_up, partner_from, axis=0), dims,
        preferred_element_type=jnp.float32,
    )
    gate_proj = both[:, :hidden]
    up_proj = both[:, hidden:]
    activated = (jax.nn.silu(gate_proj) * up_proj).astype(jnp.bfloat16)
    own_act, partner_act, act_own_from, act_partner_from = chips_then_core(activated, "rep")
    down_all = w_down[0, 0].reshape(reps, activated.shape[1], -1)
    produced = lax.dot_general(
        own_act, jnp.take(down_all, act_own_from, axis=0), dims,
        preferred_element_type=jnp.float32,
    ) + lax.dot_general(
        partner_act, jnp.take(down_all, act_partner_from, axis=0), dims,
        preferred_element_type=jnp.float32,
    )
    down_w = down_all
    out_width = down_w.shape[2]
    produced = produced.astype(jnp.bfloat16).reshape(experts, 2 * slot_depth, out_width)
    returned = lax.all_to_all(produced, "expert", split_axis=0, concat_axis=0, tiled=True)
    id_match = (chosen[:, :, None] == expert_iota[None, None, :]).astype(jnp.int32)
    row_kept = jnp.sum(id_match * admitted[:, None, :], axis=2)
    row_main = jnp.sum(id_match * main_slot[:, None, :], axis=2)
    row_spill = jnp.sum(id_match * spill_slot[:, None, :], axis=2)
    row_other = jnp.sum(id_match * spill_row[None, None, :], axis=2)
    target = jnp.where(row_kept > 0, chosen, row_other)
    slot_pick = jnp.where(row_kept > 0, row_main, slot_depth + row_spill)
    row_index = target * (2 * slot_depth) + slot_pick
    picked = jnp.take(returned.reshape(-1, out_width), row_index.reshape(-1), axis=0).reshape(
        tok_rows, top_count, out_width
    )
    combined = jnp.sum(route_weight[0][:, :, None] * picked.astype(jnp.float32), axis=1).astype(
        jnp.bfloat16
    )
    forwarded = passed_along(combined, "section", 1)
    return forwarded[None]


def solution(mesh):
    in_specs = (
        P("section", "expert", "rep"),
        P("section", "expert", None),
        P("section", "expert", None),
        P("section", "expert"),
        P(),
        P("section", None),
        P("section", "expert", None, "rep"),
        P("section", "expert", None, "rep"),
        P("section", "expert", None, "rep"),
    )
    out_specs = P("section", "expert", "rep")
    return jax.shard_map(local, mesh=mesh, in_specs=in_specs, out_specs=out_specs, check_vma=False)
```

```python
import jax
import jax.numpy as jnp
from jax import lax
from jax.sharding import PartitionSpec as P


def passed_along(value, axis, steps):
    count = lax.axis_size(axis)
    pairs = [(source, (source + steps) % count) for source in range(count)]
    return lax.ppermute(value, axis, pairs)


def gathered(value, axis):
    count = lax.axis_size(axis)
    pieces = [value]
    for shift in range(1, count):
        pairs = [(source, (source + shift) % count) for source in range(count)]
        pieces.append(lax.ppermute(value, axis, pairs))
    return pieces


def chips_then_core(value, axis):
    count = lax.axis_size(axis)
    me = lax.axis_index(axis)
    pieces = [value]
    origins = [me]
    for shift in range(2, count, 2):
        pairs = [(source, (source + shift) % count) for source in range(count)]
        pieces.append(lax.ppermute(value, axis, pairs))
        origins.append((me - shift) % count)
    bundle = jnp.stack(pieces)
    swapped = lax.ppermute(bundle, axis, [(source, source ^ 1) for source in range(count)])
    origins = jnp.stack(origins)
    return bundle, swapped, origins, origins ^ 1


def relayed_chips_then_core(value, axis):
    count = lax.axis_size(axis)
    me = lax.axis_index(axis)
    up_pairs = [(source, (source + 2) % count) for source in range(count)]
    down_pairs = [(source, (source - 2) % count) for source in range(count)]
    from_below = lax.ppermute(value, axis, up_pairs)
    from_above = lax.ppermute(value, axis, down_pairs)
    half = value.shape[0] // 2
    far_low = lax.ppermute(from_below[:half], axis, up_pairs)
    far_high = lax.ppermute(from_above[half:], axis, down_pairs)
    far = jnp.concatenate([far_low, far_high], axis=0)
    bundle = jnp.stack([value, from_below, from_above, far])
    swapped = lax.ppermute(bundle, axis, [(source, source ^ 1) for source in range(count)])
    origins = jnp.stack([me, (me - 2) % count, (me + 2) % count, (me + 4) % count])
    return bundle, swapped, origins, origins ^ 1


def paired_gather(value, axis):
    count = lax.axis_size(axis)
    me = lax.axis_index(axis)
    partner = lax.ppermute(value, axis, [(source, source ^ 1) for source in range(count)])
    pair = jnp.stack([value, partner])
    pieces = [value, partner]
    origins = [me, me ^ 1]
    for shift in range(2, count, 2):
        pairs = [(source, (source + shift) % count) for source in range(count)]
        moved = lax.ppermute(pair, axis, pairs)
        origin = (me - shift) % count
        pieces.extend([moved[0], moved[1]])
        origins.extend([origin, origin ^ 1])
    return pieces, jnp.stack(origins)


def arrival_order(weight, axis):
    count = lax.axis_size(axis)
    me = lax.axis_index(axis)
    origin = (me - jnp.arange(count, dtype=jnp.int32)) % count
    return jnp.take(weight, origin, axis=0)


def earlier(counts):
    tok_rows = counts.shape[0]
    iota = jnp.arange(tok_rows, dtype=jnp.int32)
    before = (iota[None, :] < iota[:, None]).astype(jnp.bfloat16)
    return jnp.dot(
        before, counts.astype(jnp.bfloat16), preferred_element_type=jnp.float32
    ).astype(jnp.int32)


def admission(chosen, language, capacity, experts):
    lang_count = capacity.shape[0]
    tok_rows = chosen.shape[0]
    hit_table = jnp.sum(
        (chosen[:, :, None] == jnp.arange(experts, dtype=jnp.int32)[None, None, :]).astype(
            jnp.int32
        ),
        axis=1,
    )
    lang_hot = (language[:, None] == jnp.arange(lang_count, dtype=jnp.int32)[None, :]).astype(
        jnp.int32
    )
    iota = jnp.arange(tok_rows, dtype=jnp.int32)
    same_before = ((language[None, :] == language[:, None]) & (iota[None, :] < iota[:, None])).astype(
        jnp.bfloat16
    )
    place_rank = jnp.dot(
        same_before, hit_table.astype(jnp.bfloat16), preferred_element_type=jnp.float32
    ).astype(jnp.int32)
    allowance = jnp.sum(lang_hot[:, :, None] * capacity[None, :, :], axis=1)
    admitted = hit_table * (place_rank < allowance).astype(jnp.int32)
    return (hit_table, admitted)


def slot_sources(markers, slot_table, slot_depth):
    tok_rows = markers.shape[0]
    selected = markers[:, :, None] * (
        slot_table[:, :, None] == jnp.arange(slot_depth, dtype=jnp.int32)[None, None, :]
    ).astype(jnp.int32)
    positions = jnp.arange(tok_rows, dtype=jnp.int32)[:, None, None]
    source = jnp.sum(selected * positions, axis=0)
    filled = jnp.sum(selected, axis=0)
    return jnp.where(filled > 0, source, tok_rows)


def local(tokens, expert_ids, route_weight, language, capacity, spill_table, w_gate, w_up, w_down):
    experts = lax.axis_size("expert")
    reps = lax.axis_size("rep")
    chosen = expert_ids[0]
    spill_row = spill_table[0]
    tok_rows, top_count = chosen.shape
    slot_depth = min(tok_rows, max(2, 5 * tok_rows * top_count // (4 * experts)))
    expert_iota = jnp.arange(experts, dtype=jnp.int32)
    hit_table, admitted = admission(chosen, language[0], capacity, experts)
    spilled = hit_table - admitted
    main_slot = earlier(admitted)
    spill_slot = earlier(spilled)
    spill_move = (spill_row[:, None] == expert_iota[None, :]).astype(jnp.int32)
    spill_marks = jnp.sum(spilled[:, :, None] * spill_move[None, :, :], axis=1)
    spill_places = jnp.sum((spill_slot * spilled)[:, :, None] * spill_move[None, :, :], axis=1)
    rows_local = tokens[0]
    feat_width = rows_local.shape[1]
    slot_iota = jnp.arange(slot_depth, dtype=jnp.int32)
    main_picks = admitted.T[:, None, :] * (main_slot.T[:, None, :] == slot_iota[None, :, None])
    spill_picks = spill_marks.T[:, None, :] * (
        spill_places.T[:, None, :] == slot_iota[None, :, None]
    )
    picks = jnp.concatenate([main_picks, spill_picks], axis=1).astype(rows_local.dtype)
    outgoing = jnp.einsum(
        "xjt,tf->xjf", picks, rows_local, preferred_element_type=jnp.float32
    ).astype(rows_local.dtype)
    arrived = lax.all_to_all(outgoing, "expert", split_axis=0, concat_axis=0, tiled=True)
    flattened = arrived.reshape(-1, feat_width)
    own_feats, partner_feats, own_from, partner_from = relayed_chips_then_core(flattened, "rep")
    hidden = w_gate.shape[3]
    gate_up = jnp.concatenate(
        [w_gate[0, 0].reshape(reps, feat_width, -1), w_up[0, 0].reshape(reps, feat_width, -1)],
        axis=2,
    )
    dims = (((0, 2), (0, 1)), ((), ()))
    both = lax.dot_general(
        own_feats, jnp.take(gate_up, own_from, axis=0), dims,
        preferred_element_type=jnp.float32,
    ) + lax.dot_general(
        partner_feats, jnp.take(gate_up, partner_from, axis=0), dims,
        preferred_element_type=jnp.float32,
    )
    gate_proj = both[:, :hidden]
    up_proj = both[:, hidden:]
    activated = (jax.nn.silu(gate_proj) * up_proj).astype(jnp.bfloat16)
    own_act, partner_act, act_own_from, act_partner_from = chips_then_core(activated, "rep")
    down_all = w_down[0, 0].reshape(reps, activated.shape[1], -1)
    produced = lax.dot_general(
        own_act, jnp.take(down_all, act_own_from, axis=0), dims,
        preferred_element_type=jnp.float32,
    ) + lax.dot_general(
        partner_act, jnp.take(down_all, act_partner_from, axis=0), dims,
        preferred_element_type=jnp.float32,
    )
    down_w = down_all
    out_width = down_w.shape[2]
    produced = produced.astype(jnp.bfloat16).reshape(experts, 2 * slot_depth, out_width)
    returned = lax.all_to_all(produced, "expert", split_axis=0, concat_axis=0, tiled=True)
    id_match = (chosen[:, :, None] == expert_iota[None, None, :]).astype(jnp.int32)
    row_kept = jnp.sum(id_match * admitted[:, None, :], axis=2)
    row_main = jnp.sum(id_match * main_slot[:, None, :], axis=2)
    row_spill = jnp.sum(id_match * spill_slot[:, None, :], axis=2)
    row_other = jnp.sum(id_match * spill_row[None, None, :], axis=2)
    target = jnp.where(row_kept > 0, chosen, row_other)
    slot_pick = jnp.where(row_kept > 0, row_main, slot_depth + row_spill)
    row_index = target * (2 * slot_depth) + slot_pick
    picked = jnp.take(returned.reshape(-1, out_width), row_index.reshape(-1), axis=0).reshape(
        tok_rows, top_count, out_width
    )
    combined = jnp.sum(route_weight[0][:, :, None] * picked.astype(jnp.float32), axis=1).astype(
        jnp.bfloat16
    )
    forwarded = passed_along(combined, "section", 1)
    return forwarded[None]


def solution(mesh):
    in_specs = (
        P("section", "expert", "rep"),
        P("section", "expert", None),
        P("section", "expert", None),
        P("section", "expert"),
        P(),
        P("section", None),
        P("section", "expert", None, "rep"),
        P("section", "expert", None, "rep"),
        P("section", "expert", None, "rep"),
    )
    out_specs = P("section", "expert", "rep")
    return jax.shard_map(local, mesh=mesh, in_specs=in_specs, out_specs=out_specs, check_vma=False)
```

```python
import jax
import jax.numpy as jnp
from jax import lax
from jax.sharding import PartitionSpec as P


def passed_along(value, axis, steps):
    count = lax.axis_size(axis)
    pairs = [(source, (source + steps) % count) for source in range(count)]
    return lax.ppermute(value, axis, pairs)


def gathered(value, axis):
    count = lax.axis_size(axis)
    pieces = [value]
    for shift in range(1, count):
        pairs = [(source, (source + shift) % count) for source in range(count)]
        pieces.append(lax.ppermute(value, axis, pairs))
    return pieces


def chips_then_core(value, axis):
    count = lax.axis_size(axis)
    me = lax.axis_index(axis)
    pieces = [value]
    origins = [me]
    for shift in range(2, count, 2):
        pairs = [(source, (source + shift) % count) for source in range(count)]
        pieces.append(lax.ppermute(value, axis, pairs))
        origins.append((me - shift) % count)
    bundle = jnp.stack(pieces)
    swapped = lax.ppermute(bundle, axis, [(source, source ^ 1) for source in range(count)])
    origins = jnp.stack(origins)
    return bundle, swapped, origins, origins ^ 1


def relayed_chips_then_core(value, axis):
    count = lax.axis_size(axis)
    me = lax.axis_index(axis)
    up_pairs = [(source, (source + 2) % count) for source in range(count)]
    down_pairs = [(source, (source - 2) % count) for source in range(count)]
    from_below = lax.ppermute(value, axis, up_pairs)
    from_above = lax.ppermute(value, axis, down_pairs)
    half = value.shape[0] // 2
    far_low = lax.ppermute(from_below[:half], axis, up_pairs)
    far_high = lax.ppermute(from_above[half:], axis, down_pairs)
    far = jnp.concatenate([far_low, far_high], axis=0)
    bundle = jnp.stack([value, from_below, from_above, far])
    swapped = lax.ppermute(bundle, axis, [(source, source ^ 1) for source in range(count)])
    origins = jnp.stack([me, (me - 2) % count, (me + 2) % count, (me + 4) % count])
    return bundle, swapped, origins, origins ^ 1


def paired_gather(value, axis):
    count = lax.axis_size(axis)
    me = lax.axis_index(axis)
    partner = lax.ppermute(value, axis, [(source, source ^ 1) for source in range(count)])
    pair = jnp.stack([value, partner])
    pieces = [value, partner]
    origins = [me, me ^ 1]
    for shift in range(2, count, 2):
        pairs = [(source, (source + shift) % count) for source in range(count)]
        moved = lax.ppermute(pair, axis, pairs)
        origin = (me - shift) % count
        pieces.extend([moved[0], moved[1]])
        origins.extend([origin, origin ^ 1])
    return pieces, jnp.stack(origins)


def arrival_order(weight, axis):
    count = lax.axis_size(axis)
    me = lax.axis_index(axis)
    origin = (me - jnp.arange(count, dtype=jnp.int32)) % count
    return jnp.take(weight, origin, axis=0)


def admission(chosen, language, capacity, experts):
    lang_count = capacity.shape[0]
    hit_table = jnp.sum(
        (chosen[:, :, None] == jnp.arange(experts, dtype=jnp.int32)[None, None, :]).astype(
            jnp.int32
        ),
        axis=1,
    )
    lang_hot = (language[:, None] == jnp.arange(lang_count, dtype=jnp.int32)[None, :]).astype(
        jnp.int32
    )
    lang_hits = lang_hot[:, :, None] * hit_table[:, None, :]
    before = jnp.cumsum(lang_hits, axis=0) - lang_hits
    place_rank = jnp.sum(before * lang_hot[:, :, None], axis=1)
    allowance = jnp.sum(lang_hot[:, :, None] * capacity[None, :, :], axis=1)
    admitted = hit_table * (place_rank < allowance).astype(jnp.int32)
    return (hit_table, admitted)


def slot_sources(markers, slot_table, slot_depth):
    tok_rows = markers.shape[0]
    selected = markers[:, :, None] * (
        slot_table[:, :, None] == jnp.arange(slot_depth, dtype=jnp.int32)[None, None, :]
    ).astype(jnp.int32)
    positions = jnp.arange(tok_rows, dtype=jnp.int32)[:, None, None]
    source = jnp.sum(selected * positions, axis=0)
    filled = jnp.sum(selected, axis=0)
    return jnp.where(filled > 0, source, tok_rows)


def local(tokens, expert_ids, route_weight, language, capacity, spill_table, w_gate, w_up, w_down):
    experts = lax.axis_size("expert")
    reps = lax.axis_size("rep")
    chosen = expert_ids[0]
    spill_row = spill_table[0]
    tok_rows, top_count = chosen.shape
    slot_depth = min(tok_rows, max(2, 5 * tok_rows * top_count // (4 * experts)))
    expert_iota = jnp.arange(experts, dtype=jnp.int32)
    hit_table, admitted = admission(chosen, language[0], capacity, experts)
    spilled = hit_table - admitted
    main_slot = jnp.cumsum(admitted, axis=0) - admitted
    spill_slot = jnp.cumsum(spilled, axis=0) - spilled
    spill_move = (spill_row[:, None] == expert_iota[None, :]).astype(jnp.int32)
    spill_marks = jnp.sum(spilled[:, :, None] * spill_move[None, :, :], axis=1)
    spill_places = jnp.sum((spill_slot * spilled)[:, :, None] * spill_move[None, :, :], axis=1)
    rows_local = tokens[0]
    feat_width = rows_local.shape[1]
    slot_iota = jnp.arange(slot_depth, dtype=jnp.int32)
    main_picks = admitted.T[:, None, :] * (main_slot.T[:, None, :] == slot_iota[None, :, None])
    spill_picks = spill_marks.T[:, None, :] * (
        spill_places.T[:, None, :] == slot_iota[None, :, None]
    )
    picks = jnp.concatenate([main_picks, spill_picks], axis=1).astype(rows_local.dtype)
    outgoing = jnp.einsum(
        "xjt,tf->xjf", picks, rows_local, preferred_element_type=jnp.float32
    ).astype(rows_local.dtype)
    arrived = lax.all_to_all(outgoing, "expert", split_axis=0, concat_axis=0, tiled=True)
    flattened = arrived.reshape(-1, feat_width)
    own_feats, partner_feats, own_from, partner_from = relayed_chips_then_core(flattened, "rep")
    hidden = w_gate.shape[3]
    gate_up = jnp.concatenate(
        [w_gate[0, 0].reshape(reps, feat_width, -1), w_up[0, 0].reshape(reps, feat_width, -1)],
        axis=2,
    )
    dims = (((0, 2), (0, 1)), ((), ()))
    both = lax.dot_general(
        own_feats, jnp.take(gate_up, own_from, axis=0), dims,
        preferred_element_type=jnp.float32,
    ) + lax.dot_general(
        partner_feats, jnp.take(gate_up, partner_from, axis=0), dims,
        preferred_element_type=jnp.float32,
    )
    gate_proj = both[:, :hidden]
    up_proj = both[:, hidden:]
    activated = (jax.nn.silu(gate_proj) * up_proj).astype(jnp.bfloat16)
    own_act, partner_act, act_own_from, act_partner_from = chips_then_core(activated, "rep")
    down_all = w_down[0, 0].reshape(reps, activated.shape[1], -1)
    produced = lax.dot_general(
        own_act, jnp.take(down_all, act_own_from, axis=0), dims,
        preferred_element_type=jnp.float32,
    ) + lax.dot_general(
        partner_act, jnp.take(down_all, act_partner_from, axis=0), dims,
        preferred_element_type=jnp.float32,
    )
    down_w = down_all
    out_width = down_w.shape[2]
    produced = produced.astype(jnp.bfloat16).reshape(experts, 2 * slot_depth, out_width)
    returned = lax.all_to_all(produced, "expert", split_axis=0, concat_axis=0, tiled=True)
    id_match = (chosen[:, :, None] == expert_iota[None, None, :]).astype(jnp.int32)
    row_kept = jnp.sum(id_match * admitted[:, None, :], axis=2)
    row_main = jnp.sum(id_match * main_slot[:, None, :], axis=2)
    row_spill = jnp.sum(id_match * spill_slot[:, None, :], axis=2)
    row_other = jnp.sum(id_match * spill_row[None, None, :], axis=2)
    target = jnp.where(row_kept > 0, chosen, row_other)
    slot_pick = jnp.where(row_kept > 0, row_main, slot_depth + row_spill)
    row_index = target * (2 * slot_depth) + slot_pick
    flat_returned = returned.reshape(-1, out_width)
    row_pick = (
        row_index[:, :, None] == jnp.arange(flat_returned.shape[0], dtype=jnp.int32)[None, None, :]
    ).astype(flat_returned.dtype)
    picked = jnp.einsum(
        "tks,sf->tkf", row_pick, flat_returned, preferred_element_type=jnp.float32
    )
    combined = jnp.sum(route_weight[0][:, :, None] * picked, axis=1).astype(jnp.bfloat16)
    forwarded = passed_along(combined, "section", 1)
    return forwarded[None]


def solution(mesh):
    in_specs = (
        P("section", "expert", "rep"),
        P("section", "expert", None),
        P("section", "expert", None),
        P("section", "expert"),
        P(),
        P("section", None),
        P("section", "expert", None, "rep"),
        P("section", "expert", None, "rep"),
        P("section", "expert", None, "rep"),
    )
    out_specs = P("section", "expert", "rep")
    return jax.shard_map(local, mesh=mesh, in_specs=in_specs, out_specs=out_specs, check_vma=False)
```
